256 devices in a mesh: member: 8 (over z_hi, core), tile: 32 (over y, x, z_lo).
Axes of the slice: x: 4, y: 4, z: 8 (z_hi: 4, z_lo: 2; z = z_hi * 2 + z_lo), core: 2. Of those that a mesh axis runs over, the one named last changes fastest.
Arguments:
- upsampled_coarse: bfloat16 [128, 32, 256], P('tile'), may hold values from -6 to 6
- target: bfloat16 [128, 32, 256], P('tile'), may hold values from -6 to 6
- seeds: int32 [16], P('member'), may hold values from 0 to 63
- band_row: int32 [1], replicated, may hold values from 0 to 1920
- noise_bank: float32 [64, 16], replicated, may hold values from -5 to 5
- cond_weight: float32 [16, 256], replicated, may hold values from -1.5 to 1.5
- conv_in: bfloat16 [3, 3, 32, 128], replicated, may hold values from -0.375 to 0.375
- conv_mid: bfloat16 [3, 3, 128, 128], replicated, may hold values from -0.1875 to 0.1875
- conv_out: bfloat16 [3, 3, 128, 128], replicated, may hold values from -0.1875 to 0.1875
- head_weight: bfloat16 [128, 32], replicated, may hold values from -0.5 to 0.5
- per_quantity_offset: float32 [32], replicated, may hold values from -3 to 3
Outputs:
- crps_map: float32 [128, 32, 256], P('tile', 'member')
- conv_grad: float32 [3, 3, 128, 128], replicated
- head_grad: float32 [128, 32], replicated
- bias_grad: float32 [32], replicated
The draws below stay inside these ranges and needn't reach their ends.
Inputs may be any that keep to these rules, and one draw needn't show every extreme that they name: `band_row`: the band lies inside the grid.
All inputs are finite; a program needn't handle non-finite values.
Results may differ from the reference program's by a relative error of at most 0.0015.
Values may be sent and summed in bfloat16 or wider, within the bound.
No kernel may reach another device: no remote copies, remote signals or barrier semaphores. Data moves between devices by JAX's collectives and lax.ppermute only.
A program may use at most 64 MiB of HBM per device.

```python
import math
import jax
import jax.numpy as jnp
from jax import lax

VARS = 32
CHANNELS = 128
NOISE = 16
NBANK = 64
GRID_ROWS = 2048
COLS = 256
MEMBERS = 16
ROWS = 128


def plant(drawn, stream_key, least, top_value):
    longest = drawn.shape.index(max(drawn.shape))
    spots = []
    for shift in (0, 1):
        where = [jax.random.randint(jax.random.fold_in(stream_key, axis), (), 0, length) for axis, length in enumerate(drawn.shape)]
        where[longest] = (where[longest] + shift) % drawn.shape[longest]
        spots.append(tuple(where))
    return drawn.at[spots[0]].set(least).at[spots[1]].set(top_value)


def block_scale(key, dims, pieces, least, largest):
    def one(position, parts):
        steps = jax.random.uniform(jax.random.fold_in(jax.random.fold_in(key, 6), position), (parts,), jnp.float32, least / len(pieces), largest / len(pieces))
        return jnp.repeat(jnp.exp(steps), dims[position] // parts).reshape((-1,) + (1,) * (len(dims) - position - 1))

    level = one(*pieces[0])
    for cut in pieces[1:]:
        level = level * one(*cut)
    return level


def bell_draw(own_key, dims, width, bound, shards=(), kind=jnp.bfloat16):
    entries = jax.random.normal(own_key, dims, jnp.float32) * width
    if len(shards) > 0:
        entries = block_scale(own_key, dims, shards, -0.22, 0.18) * entries
    return jnp.clip(entries, min=-bound, max=bound).astype(kind)


def setup_inputs(seed: int = 0) -> dict:
    key_list = jax.random.split(jax.random.key(seed), 12)
    upsampled_coarse = bell_draw(key_list[0], (ROWS, VARS, COLS), 1.0, 6.0, ((0, 32),))
    target = bell_draw(key_list[1], (ROWS, VARS, COLS), 1.0, 6.0, ((0, 32),))
    seeds = plant(jax.random.randint(key_list[2], (MEMBERS,), 0, NBANK), jax.random.fold_in(key_list[2], 1), 0, NBANK - 1).astype(jnp.int32)
    band_row = jax.random.randint(key_list[3], (1,), 0, GRID_ROWS - ROWS + 1).astype(jnp.int32)
    noise_bank = bell_draw(key_list[4], (NBANK, NOISE), 1.0, 5.0, (), jnp.float32)
    cond_weight = bell_draw(key_list[5], (NOISE, 2 * CHANNELS), NOISE ** -0.5, 1.5, (), jnp.float32)
    conv_in = bell_draw(key_list[6], (3, 3, VARS, CHANNELS), (9 * VARS) ** -0.5, 0.375)
    conv_mid = bell_draw(key_list[7], (3, 3, CHANNELS, CHANNELS), (9 * CHANNELS) ** -0.5, 0.1875)
    conv_out = bell_draw(key_list[8], (3, 3, CHANNELS, CHANNELS), (9 * CHANNELS) ** -0.5, 0.1875)
    head_weight = bell_draw(key_list[9], (CHANNELS, VARS), CHANNELS ** -0.5, 0.5)
    per_quantity_offset = bell_draw(key_list[10], (VARS,), 0.5, 3.0, (), jnp.float32)
    return dict(upsampled_coarse=upsampled_coarse, target=target, seeds=seeds, band_row=band_row, noise_bank=noise_bank, cond_weight=cond_weight, conv_in=conv_in, conv_mid=conv_mid, conv_out=conv_out, head_weight=head_weight, per_quantity_offset=per_quantity_offset)


def conv_three(field, kernel):
    row_count = field.shape[0]
    col_count = field.shape[1]
    padded = jnp.pad(field, ((1, 1), (1, 1), (0, 0))).astype(jnp.float32)
    kernel_wide = kernel.astype(jnp.float32)
    summed = jnp.zeros((row_count, col_count, kernel.shape[3]), jnp.float32)
    for i in range(3):
        for j in range(3):
            summed = summed + jnp.einsum('rwc,cd->rwd', padded[i:i + row_count, j:j + col_count], kernel_wide[i, j])
    return summed

def condition(base, cond_scale, cond_shift):
    average = lax.optimization_barrier(jnp.mean(base, axis=-1, keepdims=True))
    centred = base - average
    spread = lax.optimization_barrier(jnp.mean(centred * centred, axis=-1, keepdims=True))
    normed = centred * lax.rsqrt(spread + 1e-05)
    return jax.nn.gelu(normed * (1.0 + cond_scale) + cond_shift).astype(jnp.bfloat16)

def reference(upsampled_coarse, target, seeds, band_row, noise_bank, cond_weight, conv_in, conv_mid, conv_out, head_weight, per_quantity_offset):
    channels = conv_mid.shape[3]
    base = conv_three(jnp.transpose(upsampled_coarse, (0, 2, 1)), conv_in)
    noise_vec = noise_bank[seeds]
    random_latent_gain = jnp.dot(noise_vec, cond_weight, precision=lax.Precision.HIGHEST)

    def evaluate_sample_network(perturbation_line):
        first_hidden = condition(base, perturbation_line[:channels], perturbation_line[channels:])
        latent_layer_two = jax.nn.gelu(conv_three(first_hidden, conv_mid)).astype(jnp.bfloat16)
        final_linear_response = conv_three(latent_layer_two, conv_out)
        latent_layer_three = (first_hidden.astype(jnp.float32) + jax.nn.gelu(final_linear_response)).astype(jnp.bfloat16)
        final_layer_result = jnp.einsum('rwc,cv->rvw', latent_layer_three.astype(jnp.float32), head_weight.astype(jnp.float32))
        sample_prediction = (upsampled_coarse.astype(jnp.float32) + final_layer_result + per_quantity_offset[None, :, None]).astype(jnp.bfloat16)
        return (latent_layer_two, final_linear_response, latent_layer_three, sample_prediction)
    predicted_fields_list = lax.map(lambda perturbation_line: evaluate_sample_network(perturbation_line)[3], random_latent_gain)
    sample_group_predictions = predicted_fields_list.astype(jnp.float32)
    truth = target.astype(jnp.float32)
    member_count = sample_group_predictions.shape[0]

    def pair_terms(member_index):
        differ = member_index[None] - sample_group_predictions
        return (lax.optimization_barrier(jnp.sum(jnp.abs(differ), axis=0)), lax.optimization_barrier(jnp.sum(jnp.sign(differ), axis=0)))
    abs_sums, sign_sums = lax.map(pair_terms, sample_group_predictions)
    crps_map = lax.optimization_barrier(jnp.mean(jnp.abs(sample_group_predictions - truth[None]), axis=0)) - lax.optimization_barrier(jnp.sum(abs_sums, axis=0)) / (2 * member_count * (member_count - 1))
    row_global = band_row[0] + jnp.arange(ROWS, dtype=jnp.int32)
    latitude = math.pi * (row_global.astype(jnp.float32) + 0.5) / GRID_ROWS - math.pi / 2
    row_factor = jnp.cos(latitude) / (ROWS * COLS)
    cotangent = (row_factor[None, :, None, None] * (jnp.sign(sample_group_predictions - truth[None]) / member_count - sign_sums / (member_count * (member_count - 1)))).astype(jnp.bfloat16)

    def member_grads(pair_in):
        perturbation_line, cot_member = pair_in
        latent_layer_two, final_linear_response, latent_layer_three, unused = evaluate_sample_network(perturbation_line)
        cot_wide = cot_member.astype(jnp.float32)
        head_part = jnp.einsum('rwc,rvw->cv', latent_layer_three.astype(jnp.float32), cot_wide)
        bias_part = lax.optimization_barrier(jnp.sum(cot_wide, axis=(0, 2)))
        back = jnp.einsum('rvw,cv->rwc', cot_wide, head_weight.astype(jnp.float32))
        unused_out, pullback = jax.vjp(jax.nn.gelu, final_linear_response)
        d_pre = pullback(back)[0].astype(jnp.bfloat16).astype(jnp.float32)
        padded = jnp.pad(latent_layer_two, ((1, 1), (1, 1), (0, 0))).astype(jnp.float32)
        row_count = d_pre.shape[0]
        col_count = d_pre.shape[1]
        rows_of = []
        for i in range(3):
            cols_of = []
            for j in range(3):
                cols_of.append(jnp.einsum('rwc,rwd->cd', padded[i:i + row_count, j:j + col_count], d_pre))
            rows_of.append(jnp.stack(cols_of))
        return (jnp.stack(rows_of), head_part, bias_part)
    conv_parts, head_parts, bias_parts = lax.map(member_grads, (random_latent_gain, cotangent))
    return (crps_map, lax.optimization_barrier(jnp.sum(conv_parts, axis=0)), lax.optimization_barrier(jnp.sum(head_parts, axis=0)), lax.optimization_barrier(jnp.sum(bias_parts, axis=0)))
```

```python
import math

import jax
import jax.numpy as jnp
from jax import lax
from jax.sharding import PartitionSpec as P

GRID_ROWS = 2048


def extended(x, sides, width):
    for axis, dim in sides:
        devices, length = (lax.axis_size(axis), x.shape[dim])
        up = [(i, (i + 1) % devices) for i in range(devices - 1)]
        down = [(j, i) for i, j in up]
        last = lax.slice_in_dim(x, length - width, length, axis=dim)
        first = lax.slice_in_dim(x, 0, width, axis=dim)
        before = lax.ppermute(last, axis, up)
        after = lax.ppermute(first, axis, down)
        x = jnp.concatenate([before, x, after], axis=dim)
    return x


def input_conv(padded, kernel):
    out_rows = padded.shape[0] - 2
    col_count = padded.shape[2]
    wide = jnp.pad(padded, ((0, 0), (0, 0), (1, 1)))
    summed = jnp.zeros((out_rows, col_count, kernel.shape[3]), jnp.float32)
    for i in range(3):
        for j in range(3):
            summed = summed + jnp.einsum(
                "rkw,kc->rwc",
                wide[i : i + out_rows, :, j : j + col_count],
                kernel[i, j],
                preferred_element_type=jnp.float32,
            )
    return summed


def feature_conv(padded, kernel):
    out_rows = padded.shape[1] - 2
    col_count = padded.shape[2]
    wide = jnp.pad(padded, ((0, 0), (0, 0), (1, 1), (0, 0)))
    summed = jnp.zeros((padded.shape[0], out_rows, col_count, kernel.shape[3]), jnp.float32)
    for i in range(3):
        for j in range(3):
            summed = summed + jnp.einsum(
                "mrwc,cd->mrwd",
                wide[:, i : i + out_rows, j : j + col_count],
                kernel[i, j],
                preferred_element_type=jnp.float32,
            )
    return summed


def condition(base, cond_scale, cond_shift):
    average = jnp.mean(base, axis=-1, keepdims=True)
    centred = base - average
    spread = jnp.mean(centred * centred, axis=-1, keepdims=True)
    normed = centred * lax.rsqrt(spread + 1e-05)
    mixed = normed[None] * (1.0 + cond_scale[:, None, None, :]) + cond_shift[:, None, None, :]
    return jax.nn.gelu(mixed).astype(jnp.bfloat16)


def abs_terms(probe, sample_group_predictions):

    def abs_single(member_index):
        return jnp.sum(jnp.abs(member_index[None] - sample_group_predictions), axis=0)

    return lax.map(abs_single, probe)


def sign_terms(probe, sample_group_predictions):

    def sign_single(member_index):
        return jnp.sum(jnp.sign(member_index[None] - sample_group_predictions), axis=0)

    return lax.map(sign_single, probe)


def all_reduce_sum(parts, axes):
    devices = 1
    for axis in axes:
        devices *= lax.axis_size(axis)
    flat = jnp.concatenate([p.reshape(-1) for p in parts])
    total = flat.shape[0]
    width = -(-total // devices)
    flat = jnp.pad(flat, (0, width * devices - total)).reshape(devices, width)
    pieces = lax.all_to_all(flat, axes, 0, 0, tiled=True)
    own = jnp.sum(pieces, axis=0, keepdims=True)
    spread = lax.all_to_all(jnp.broadcast_to(own, (devices, width)), axes, 0, 0, tiled=True)
    spread = spread.reshape(-1)
    out, at = [], 0
    for p in parts:
        out.append(spread[at : at + p.size].reshape(p.shape))
        at += p.size
    return tuple(out)


def on_device(
    upsampled_coarse,
    target,
    seeds,
    band_row,
    noise_bank,
    cond_weight,
    conv_in,
    conv_mid,
    conv_out,
    head_weight,
    per_quantity_offset,
):
    channels = conv_mid.shape[3]
    row_count = upsampled_coarse.shape[0]
    var_count = upsampled_coarse.shape[1]
    col_count = upsampled_coarse.shape[2]
    tile_count = lax.axis_size("tile")
    tile_at = lax.axis_index("tile")
    band_rows = row_count * tile_count
    selector = (seeds[:, None] == jnp.arange(noise_bank.shape[0], dtype=jnp.int32)[None]).astype(
        jnp.float32
    )
    noise_vec = jnp.dot(selector, noise_bank, precision=lax.Precision.HIGHEST)
    random_latent_gain = jnp.dot(noise_vec, cond_weight, precision=lax.Precision.HIGHEST)
    cond_scale = random_latent_gain[:, :channels]
    cond_shift = random_latent_gain[:, channels:]
    input_padded = extended(upsampled_coarse, (("tile", 0),), 1)
    first_hidden = condition(input_conv(input_padded, conv_in), cond_scale, cond_shift)
    first_padded = extended(first_hidden, (("tile", 1),), 1)
    latent_layer_two = jax.nn.gelu(feature_conv(first_padded, conv_mid)).astype(jnp.bfloat16)
    second_padded = extended(latent_layer_two, (("tile", 1),), 1)
    final_linear_response = feature_conv(second_padded, conv_out)
    latent_layer_three = (
        first_hidden.astype(jnp.float32) + jax.nn.gelu(final_linear_response)
    ).astype(jnp.bfloat16)
    final_layer_result = jnp.einsum(
        "mrwc,cv->mrvw", latent_layer_three, head_weight, preferred_element_type=jnp.float32
    )
    sample_prediction = (
        final_layer_result
        + upsampled_coarse.astype(jnp.float32)[None]
        + per_quantity_offset[None, None, :, None]
    ).astype(jnp.bfloat16)
    row_global = band_row[0] + tile_at * row_count + jnp.arange(row_count, dtype=jnp.int32)
    latitude = math.pi * (row_global.astype(jnp.float32) + 0.5) / GRID_ROWS - math.pi / 2
    row_factor = (jnp.cos(latitude) / (band_rows * col_count))[None, :, None, None]
    var_share = var_count // lax.axis_size("member")
    var_start = lax.axis_index("member") * var_share
    collected_members = lax.all_to_all(
        sample_prediction, "member", split_axis=2, concat_axis=0, tiled=True
    )
    sample_group_predictions = collected_members.astype(jnp.float32)
    member_count = sample_group_predictions.shape[0]
    truth = lax.dynamic_slice_in_dim(target, var_start, var_share, 1).astype(jnp.float32)
    abs_sums = abs_terms(sample_group_predictions, sample_group_predictions)
    sign_sums = sign_terms(sample_group_predictions, sample_group_predictions)
    crps_map = jnp.mean(jnp.abs(sample_group_predictions - truth[None]), axis=0) - jnp.sum(
        abs_sums, axis=0
    ) / (2 * member_count * (member_count - 1))
    cot_share = (
        row_factor
        * (
            jnp.sign(sample_group_predictions - truth[None]) / member_count
            - sign_sums / (member_count * (member_count - 1))
        )
    ).astype(jnp.bfloat16)
    cotangent = lax.all_to_all(cot_share, "member", split_axis=0, concat_axis=2, tiled=True)
    head_grad = jnp.einsum(
        "mrwc,mrvw->cv", latent_layer_three, cotangent, preferred_element_type=jnp.float32
    )
    bias_grad = jnp.sum(cotangent.astype(jnp.float32), axis=(0, 1, 3))
    back = jnp.einsum("mrvw,cv->mrwc", cotangent, head_weight, preferred_element_type=jnp.float32)
    unused_out, pullback = jax.vjp(jax.nn.gelu, final_linear_response)
    d_pre = pullback(back)[0].astype(jnp.bfloat16)
    second_wide = jnp.pad(second_padded, ((0, 0), (0, 0), (1, 1), (0, 0)))
    rows_of = []
    for i in range(3):
        cols_of = []
        for j in range(3):
            cols_of.append(
                jnp.einsum(
                    "mrwc,mrwd->cd",
                    second_wide[:, i : i + row_count, j : j + col_count],
                    d_pre,
                    preferred_element_type=jnp.float32,
                )
            )
        rows_of.append(jnp.stack(cols_of))
    conv_grad = jnp.stack(rows_of)
    conv_grad, head_grad, bias_grad = all_reduce_sum((conv_grad, head_grad, bias_grad), ("member", "tile"))
    return (crps_map, conv_grad, head_grad, bias_grad)


def solution(mesh):
    return jax.shard_map(
        on_device,
        mesh=mesh,
        in_specs=(
            P("tile", None, None),
            P("tile", None, None),
            P("member"),
            P(),
            P(),
            P(),
            P(),
            P(),
            P(),
            P(),
            P(),
        ),
        out_specs=(P("tile", "member", None), P(), P(), P()),
        check_vma=False,
    )
```

```python
import math

import jax
import jax.numpy as jnp
from jax import lax
from jax.sharding import PartitionSpec as P

GRID_ROWS = 2048


def extended(x, sides, width):
    for axis, dim in sides:
        devices, length = (lax.axis_size(axis), x.shape[dim])
        up = [(i, (i + 1) % devices) for i in range(devices - 1)]
        down = [(j, i) for i, j in up]
        last = lax.slice_in_dim(x, length - width, length, axis=dim)
        first = lax.slice_in_dim(x, 0, width, axis=dim)
        before = lax.ppermute(last, axis, up)
        after = lax.ppermute(first, axis, down)
        x = jnp.concatenate([before, x, after], axis=dim)
    return x


def input_conv(padded, kernel):
    out_rows = padded.shape[0] - 2
    col_count = padded.shape[2]
    wide = jnp.pad(padded, ((0, 0), (0, 0), (1, 1)))
    summed = jnp.zeros((out_rows, col_count, kernel.shape[3]), jnp.float32)
    for i in range(3):
        for j in range(3):
            summed = summed + jnp.einsum(
                "rkw,kc->rwc",
                wide[i : i + out_rows, :, j : j + col_count],
                kernel[i, j],
                preferred_element_type=jnp.float32,
            )
    return summed


def feature_conv(padded, kernel):
    out_rows = padded.shape[1] - 2
    col_count = padded.shape[2]
    wide = jnp.pad(padded, ((0, 0), (0, 0), (1, 1), (0, 0)))
    summed = jnp.zeros((padded.shape[0], out_rows, col_count, kernel.shape[3]), jnp.float32)
    for i in range(3):
        for j in range(3):
            summed = summed + jnp.einsum(
                "mrwc,cd->mrwd",
                wide[:, i : i + out_rows, j : j + col_count],
                kernel[i, j],
                preferred_element_type=jnp.float32,
            )
    return summed


def condition(base, cond_scale, cond_shift):
    average = jnp.mean(base, axis=-1, keepdims=True)
    centred = base - average
    spread = jnp.mean(centred * centred, axis=-1, keepdims=True)
    normed = centred * lax.rsqrt(spread + 1e-05)
    mixed = normed[None] * (1.0 + cond_scale[:, None, None, :]) + cond_shift[:, None, None, :]
    return jax.nn.gelu(mixed).astype(jnp.bfloat16)


def abs_terms(probe, sample_group_predictions):

    def abs_single(member_index):
        return jnp.sum(jnp.abs(member_index[None] - sample_group_predictions), axis=0)

    return lax.map(abs_single, probe)


def sign_terms(probe, sample_group_predictions):

    def sign_single(member_index):
        return jnp.sum(jnp.sign(member_index[None] - sample_group_predictions), axis=0)

    return lax.map(sign_single, probe)


def all_reduce_sum(conv_grad, head_grad, bias_grad, axes):
    devices = 1
    for axis in axes:
        devices *= lax.axis_size(axis)
    lanes = conv_grad.shape[-1]
    conv_rows = conv_grad.size // lanes
    rows = conv_rows + head_grad.shape[1] + 1
    per = -(-rows // devices)
    bias_row = jnp.pad(bias_grad, (0, lanes - bias_grad.shape[0]))[None]
    flat = jnp.concatenate(
        [
            conv_grad.reshape(conv_rows, lanes),
            head_grad.T,
            bias_row,
            jnp.zeros((per * devices - rows, lanes), jnp.float32),
        ]
    ).reshape(devices, per, lanes)
    pieces = lax.all_to_all(flat, axes, 0, 0, tiled=True)
    own = jnp.sum(pieces, axis=0, keepdims=True)
    spread = lax.all_to_all(jnp.broadcast_to(own, flat.shape), axes, 0, 0, tiled=True)
    spread = spread.reshape(per * devices, lanes)
    conv_sum = spread[:conv_rows].reshape(conv_grad.shape)
    head_sum = spread[conv_rows : conv_rows + head_grad.shape[1]].T
    bias_sum = spread[conv_rows + head_grad.shape[1], : bias_grad.shape[0]]
    return conv_sum, head_sum, bias_sum


def on_device(
    upsampled_coarse,
    target,
    seeds,
    band_row,
    noise_bank,
    cond_weight,
    conv_in,
    conv_mid,
    conv_out,
    head_weight,
    per_quantity_offset,
):
    channels = conv_mid.shape[3]
    row_count = upsampled_coarse.shape[0]
    var_count = upsampled_coarse.shape[1]
    col_count = upsampled_coarse.shape[2]
    tile_count = lax.axis_size("tile")
    tile_at = lax.axis_index("tile")
    band_rows = row_count * tile_count
    selector = (seeds[:, None] == jnp.arange(noise_bank.shape[0], dtype=jnp.int32)[None]).astype(
        jnp.float32
    )
    noise_vec = jnp.dot(selector, noise_bank, precision=lax.Precision.HIGHEST)
    random_latent_gain = jnp.dot(noise_vec, cond_weight, precision=lax.Precision.HIGHEST)
    cond_scale = random_latent_gain[:, :channels]
    cond_shift = random_latent_gain[:, channels:]
    input_padded = extended(upsampled_coarse, (("tile", 0),), 1)
    first_hidden = condition(input_conv(input_padded, conv_in), cond_scale, cond_shift)
    first_padded = extended(first_hidden, (("tile", 1),), 1)
    latent_layer_two = jax.nn.gelu(feature_conv(first_padded, conv_mid)).astype(jnp.bfloat16)
    second_padded = extended(latent_layer_two, (("tile", 1),), 1)
    final_linear_response = feature_conv(second_padded, conv_out)
    latent_layer_three = (
        first_hidden.astype(jnp.float32) + jax.nn.gelu(final_linear_response)
    ).astype(jnp.bfloat16)
    final_layer_result = jnp.einsum(
        "mrwc,cv->mrvw", latent_layer_three, head_weight, preferred_element_type=jnp.float32
    )
    sample_prediction = (
        final_layer_result
        + upsampled_coarse.astype(jnp.float32)[None]
        + per_quantity_offset[None, None, :, None]
    ).astype(jnp.bfloat16)
    row_global = band_row[0] + tile_at * row_count + jnp.arange(row_count, dtype=jnp.int32)
    latitude = math.pi * (row_global.astype(jnp.float32) + 0.5) / GRID_ROWS - math.pi / 2
    row_factor = (jnp.cos(latitude) / (band_rows * col_count))[None, :, None, None]
    var_share = var_count // lax.axis_size("member")
    var_start = lax.axis_index("member") * var_share
    collected_members = lax.all_to_all(
        sample_prediction, "member", split_axis=2, concat_axis=0, tiled=True
    )
    sample_group_predictions = collected_members.astype(jnp.float32)
    member_count = sample_group_predictions.shape[0]
    truth = lax.dynamic_slice_in_dim(target, var_start, var_share, 1).astype(jnp.float32)
    abs_sums = abs_terms(sample_group_predictions, sample_group_predictions)
    sign_sums = sign_terms(sample_group_predictions, sample_group_predictions)
    crps_map = jnp.mean(jnp.abs(sample_group_predictions - truth[None]), axis=0) - jnp.sum(
        abs_sums, axis=0
    ) / (2 * member_count * (member_count - 1))
    cot_share = (
        row_factor
        * (
            jnp.sign(sample_group_predictions - truth[None]) / member_count
            - sign_sums / (member_count * (member_count - 1))
        )
    ).astype(jnp.bfloat16)
    cotangent = lax.all_to_all(cot_share, "member", split_axis=0, concat_axis=2, tiled=True)
    head_grad = jnp.einsum(
        "mrwc,mrvw->cv", latent_layer_three, cotangent, preferred_element_type=jnp.float32
    )
    bias_grad = jnp.sum(cotangent.astype(jnp.float32), axis=(0, 1, 3))
    back = jnp.einsum("mrvw,cv->mrwc", cotangent, head_weight, preferred_element_type=jnp.float32)
    unused_out, pullback = jax.vjp(jax.nn.gelu, final_linear_response)
    d_pre = pullback(back)[0].astype(jnp.bfloat16)
    second_wide = jnp.pad(second_padded, ((0, 0), (0, 0), (1, 1), (0, 0)))
    rows_of = []
    for i in range(3):
        cols_of = []
        for j in range(3):
            cols_of.append(
                jnp.einsum(
                    "mrwc,mrwd->cd",
                    second_wide[:, i : i + row_count, j : j + col_count],
                    d_pre,
                    preferred_element_type=jnp.float32,
                )
            )
        rows_of.append(jnp.stack(cols_of))
    conv_grad = jnp.stack(rows_of)
    conv_grad, head_grad, bias_grad = all_reduce_sum(conv_grad, head_grad, bias_grad, ("member", "tile"))
    return (crps_map, conv_grad, head_grad, bias_grad)


def solution(mesh):
    return jax.shard_map(
        on_device,
        mesh=mesh,
        in_specs=(
            P("tile", None, None),
            P("tile", None, None),
            P("member"),
            P(),
            P(),
            P(),
            P(),
            P(),
            P(),
            P(),
            P(),
        ),
        out_specs=(P("tile", "member", None), P(), P(), P()),
        check_vma=False,
    )
```

```python
import math

import jax
import jax.numpy as jnp
from jax import lax
from jax.sharding import PartitionSpec as P

GRID_ROWS = 2048


def extended(x, sides, width):
    for axis, dim in sides:
        devices, length = (lax.axis_size(axis), x.shape[dim])
        up = [(i, (i + 1) % devices) for i in range(devices - 1)]
        down = [(j, i) for i, j in up]
        last = lax.slice_in_dim(x, length - width, length, axis=dim)
        first = lax.slice_in_dim(x, 0, width, axis=dim)
        before = lax.ppermute(last, axis, up)
        after = lax.ppermute(first, axis, down)
        x = jnp.concatenate([before, x, after], axis=dim)
    return x


def input_conv(padded, kernel):
    out_rows = padded.shape[0] - 2
    col_count = padded.shape[2]
    wide = jnp.pad(padded, ((0, 0), (0, 0), (1, 1)))
    summed = jnp.zeros((out_rows, col_count, kernel.shape[3]), jnp.float32)
    for i in range(3):
        for j in range(3):
            summed = summed + jnp.einsum(
                "rkw,kc->rwc",
                wide[i : i + out_rows, :, j : j + col_count],
                kernel[i, j],
                preferred_element_type=jnp.float32,
            )
    return summed


def feature_conv(padded, kernel):
    out_rows = padded.shape[1] - 2
    col_count = padded.shape[2]
    wide = jnp.pad(padded, ((0, 0), (0, 0), (1, 1), (0, 0)))
    summed = jnp.zeros((padded.shape[0], out_rows, col_count, kernel.shape[3]), jnp.float32)
    for i in range(3):
        for j in range(3):
            summed = summed + jnp.einsum(
                "mrwc,cd->mrwd",
                wide[:, i : i + out_rows, j : j + col_count],
                kernel[i, j],
                preferred_element_type=jnp.float32,
            )
    return summed


def condition(base, cond_scale, cond_shift):
    average = jnp.mean(base, axis=-1, keepdims=True)
    centred = base - average
    spread = jnp.mean(centred * centred, axis=-1, keepdims=True)
    normed = centred * lax.rsqrt(spread + 1e-05)
    mixed = normed[None] * (1.0 + cond_scale[:, None, None, :]) + cond_shift[:, None, None, :]
    return jax.nn.gelu(mixed).astype(jnp.bfloat16)


def abs_terms(probe, sample_group_predictions):

    def abs_single(member_index):
        return jnp.sum(jnp.abs(member_index[None] - sample_group_predictions), axis=0)

    return lax.map(abs_single, probe)


def sign_terms(probe, sample_group_predictions):

    def sign_single(member_index):
        return jnp.sum(jnp.sign(member_index[None] - sample_group_predictions), axis=0)

    return lax.map(sign_single, probe)


def all_reduce_sum(parts, axes):
    devices = 1
    for axis in axes:
        devices *= lax.axis_size(axis)
    flat = jnp.concatenate([p.reshape(-1) for p in parts])
    total = flat.shape[0]
    width = -(-total // devices)
    flat = jnp.pad(flat, (0, width * devices - total)).reshape(devices, width)
    pieces = lax.all_to_all(flat, axes, 0, 0, tiled=True)
    own = jnp.sum(pieces, axis=0, keepdims=True)
    spread = lax.all_to_all(jnp.broadcast_to(own, (devices, width)), axes, 0, 0, tiled=True)
    spread = spread.reshape(-1)
    out, at = [], 0
    for p in parts:
        out.append(spread[at : at + p.size].reshape(p.shape))
        at += p.size
    return tuple(out)


def on_device(
    upsampled_coarse,
    target,
    seeds,
    band_row,
    noise_bank,
    cond_weight,
    conv_in,
    conv_mid,
    conv_out,
    head_weight,
    per_quantity_offset,
):
    channels = conv_mid.shape[3]
    row_count = upsampled_coarse.shape[0]
    var_count = upsampled_coarse.shape[1]
    col_count = upsampled_coarse.shape[2]
    tile_count = lax.axis_size("tile")
    tile_at = lax.axis_index("tile")
    band_rows = row_count * tile_count
    selector = (seeds[:, None] == jnp.arange(noise_bank.shape[0], dtype=jnp.int32)[None]).astype(
        jnp.float32
    )
    noise_vec = jnp.dot(selector, noise_bank, precision=lax.Precision.HIGHEST)
    random_latent_gain = jnp.dot(noise_vec, cond_weight, precision=lax.Precision.HIGHEST)
    cond_scale = random_latent_gain[:, :channels]
    cond_shift = random_latent_gain[:, channels:]
    input_padded = extended(upsampled_coarse, (("tile", 0),), 3)
    band_at = tile_at * row_count + jnp.arange(-2, row_count + 2, dtype=jnp.int32)
    inside = ((band_at >= 0) & (band_at < band_rows))[None, :, None, None]
    first_wide = condition(input_conv(input_padded, conv_in), cond_scale, cond_shift)
    first_wide = jnp.where(inside, first_wide, jnp.zeros_like(first_wide))
    first_hidden = first_wide[:, 2 : 2 + row_count]
    second_padded = jax.nn.gelu(feature_conv(first_wide, conv_mid)).astype(jnp.bfloat16)
    second_padded = jnp.where(inside[:, 1:-1], second_padded, jnp.zeros_like(second_padded))
    final_linear_response = feature_conv(second_padded, conv_out)
    latent_layer_three = (
        first_hidden.astype(jnp.float32) + jax.nn.gelu(final_linear_response)
    ).astype(jnp.bfloat16)
    final_layer_result = jnp.einsum(
        "mrwc,cv->mrvw", latent_layer_three, head_weight, preferred_element_type=jnp.float32
    )
    sample_prediction = (
        final_layer_result
        + upsampled_coarse.astype(jnp.float32)[None]
        + per_quantity_offset[None, None, :, None]
    ).astype(jnp.bfloat16)
    row_global = band_row[0] + tile_at * row_count + jnp.arange(row_count, dtype=jnp.int32)
    latitude = math.pi * (row_global.astype(jnp.float32) + 0.5) / GRID_ROWS - math.pi / 2
    row_factor = (jnp.cos(latitude) / (band_rows * col_count))[None, :, None, None]
    var_share = var_count // lax.axis_size("member")
    var_start = lax.axis_index("member") * var_share
    collected_members = lax.all_to_all(
        sample_prediction, "member", split_axis=2, concat_axis=0, tiled=True
    )
    sample_group_predictions = collected_members.astype(jnp.float32)
    member_count = sample_group_predictions.shape[0]
    truth = lax.dynamic_slice_in_dim(target, var_start, var_share, 1).astype(jnp.float32)
    abs_sums = abs_terms(sample_group_predictions, sample_group_predictions)
    sign_sums = sign_terms(sample_group_predictions, sample_group_predictions)
    crps_map = jnp.mean(jnp.abs(sample_group_predictions - truth[None]), axis=0) - jnp.sum(
        abs_sums, axis=0
    ) / (2 * member_count * (member_count - 1))
    cot_share = (
        row_factor
        * (
            jnp.sign(sample_group_predictions - truth[None]) / member_count
            - sign_sums / (member_count * (member_count - 1))
        )
    ).astype(jnp.bfloat16)
    cotangent = lax.all_to_all(cot_share, "member", split_axis=0, concat_axis=2, tiled=True)
    head_grad = jnp.einsum(
        "mrwc,mrvw->cv", latent_layer_three, cotangent, preferred_element_type=jnp.float32
    )
    bias_grad = jnp.sum(cotangent.astype(jnp.float32), axis=(0, 1, 3))
    back = jnp.einsum("mrvw,cv->mrwc", cotangent, head_weight, preferred_element_type=jnp.float32)
    unused_out, pullback = jax.vjp(jax.nn.gelu, final_linear_response)
    d_pre = pullback(back)[0].astype(jnp.bfloat16)
    second_wide = jnp.pad(second_padded, ((0, 0), (0, 0), (1, 1), (0, 0)))
    rows_of = []
    for i in range(3):
        cols_of = []
        for j in range(3):
            cols_of.append(
                jnp.einsum(
                    "mrwc,mrwd->cd",
                    second_wide[:, i : i + row_count, j : j + col_count],
                    d_pre,
                    preferred_element_type=jnp.float32,
                )
            )
        rows_of.append(jnp.stack(cols_of))
    conv_grad = jnp.stack(rows_of)
    conv_grad, head_grad, bias_grad = all_reduce_sum((conv_grad, head_grad, bias_grad), ("member", "tile"))
    return (crps_map, conv_grad, head_grad, bias_grad)


def solution(mesh):
    return jax.shard_map(
        on_device,
        mesh=mesh,
        in_specs=(
            P("tile", None, None),
            P("tile", None, None),
            P("member"),
            P(),
            P(),
            P(),
            P(),
            P(),
            P(),
            P(),
            P(),
        ),
        out_specs=(P("tile", "member", None), P(), P(), P()),
        check_vma=False,
    )
```

```python
import math

import jax
import jax.numpy as jnp
from jax import lax
from jax.sharding import PartitionSpec as P

GRID_ROWS = 2048


def extended(x, sides, width):
    for axis, dim in sides:
        devices, length = (lax.axis_size(axis), x.shape[dim])
        up = [(i, (i + 1) % devices) for i in range(devices - 1)]
        down = [(j, i) for i, j in up]
        last = lax.slice_in_dim(x, length - width, length, axis=dim)
        first = lax.slice_in_dim(x, 0, width, axis=dim)
        before = lax.ppermute(last, axis, up)
        after = lax.ppermute(first, axis, down)
        x = jnp.concatenate([before, x, after], axis=dim)
    return x


def input_conv(padded, kernel):
    out_rows = padded.shape[0] - 2
    col_count = padded.shape[2]
    wide = jnp.pad(padded, ((0, 0), (0, 0), (1, 1)))
    summed = jnp.zeros((out_rows, col_count, kernel.shape[3]), jnp.float32)
    for i in range(3):
        for j in range(3):
            summed = summed + jnp.einsum(
                "rkw,kc->rwc",
                wide[i : i + out_rows, :, j : j + col_count],
                kernel[i, j],
                preferred_element_type=jnp.float32,
            )
    return summed


def feature_conv(padded, kernel):
    out_rows = padded.shape[1] - 2
    col_count = padded.shape[2]
    wide = jnp.pad(padded, ((0, 0), (0, 0), (1, 1), (0, 0)))
    summed = jnp.zeros((padded.shape[0], out_rows, col_count, kernel.shape[3]), jnp.float32)
    for i in range(3):
        for j in range(3):
            summed = summed + jnp.einsum(
                "mrwc,cd->mrwd",
                wide[:, i : i + out_rows, j : j + col_count],
                kernel[i, j],
                preferred_element_type=jnp.float32,
            )
    return summed


def condition(base, cond_scale, cond_shift):
    average = jnp.mean(base, axis=-1, keepdims=True)
    centred = base - average
    spread = jnp.mean(centred * centred, axis=-1, keepdims=True)
    normed = centred * lax.rsqrt(spread + 1e-05)
    mixed = normed[None] * (1.0 + cond_scale[:, None, None, :]) + cond_shift[:, None, None, :]
    return jax.nn.gelu(mixed).astype(jnp.bfloat16)


def abs_terms(probe, sample_group_predictions):

    def abs_single(member_index):
        return jnp.sum(jnp.abs(member_index[None] - sample_group_predictions), axis=0)

    return lax.map(abs_single, probe)


def sign_terms(probe, sample_group_predictions):

    def sign_single(member_index):
        return jnp.sum(jnp.sign(member_index[None] - sample_group_predictions), axis=0)

    return lax.map(sign_single, probe)


def all_reduce_sum(parts, axes):
    devices = 1
    for axis in axes:
        devices *= lax.axis_size(axis)
    flat = jnp.concatenate([p.reshape(-1) for p in parts])
    total = flat.shape[0]
    width = -(-total // (devices * 128)) * 128
    flat = jnp.pad(flat, (0, width * devices - total)).reshape(devices, width)
    pieces = lax.all_to_all(flat, axes, 0, 0, tiled=True)
    own = jnp.sum(pieces, axis=0, keepdims=True)
    spread = lax.all_to_all(jnp.broadcast_to(own, (devices, width)), axes, 0, 0, tiled=True)
    spread = spread.reshape(-1)
    out, at = [], 0
    for p in parts:
        out.append(spread[at : at + p.size].reshape(p.shape))
        at += p.size
    return tuple(out)


def on_device(
    upsampled_coarse,
    target,
    seeds,
    band_row,
    noise_bank,
    cond_weight,
    conv_in,
    conv_mid,
    conv_out,
    head_weight,
    per_quantity_offset,
):
    channels = conv_mid.shape[3]
    row_count = upsampled_coarse.shape[0]
    var_count = upsampled_coarse.shape[1]
    col_count = upsampled_coarse.shape[2]
    tile_count = lax.axis_size("tile")
    tile_at = lax.axis_index("tile")
    band_rows = row_count * tile_count
    selector = (seeds[:, None] == jnp.arange(noise_bank.shape[0], dtype=jnp.int32)[None]).astype(
        jnp.float32
    )
    noise_vec = jnp.dot(selector, noise_bank, precision=lax.Precision.HIGHEST)
    random_latent_gain = jnp.dot(noise_vec, cond_weight, precision=lax.Precision.HIGHEST)
    cond_scale = random_latent_gain[:, :channels]
    cond_shift = random_latent_gain[:, channels:]
    input_padded = extended(upsampled_coarse, (("tile", 0),), 3)
    band_at = tile_at * row_count + jnp.arange(-2, row_count + 2, dtype=jnp.int32)
    inside = ((band_at >= 0) & (band_at < band_rows))[None, :, None, None]
    first_wide = condition(input_conv(input_padded, conv_in), cond_scale, cond_shift)
    first_wide = jnp.where(inside, first_wide, jnp.zeros_like(first_wide))
    first_hidden = first_wide[:, 2 : 2 + row_count]
    second_padded = jax.nn.gelu(feature_conv(first_wide, conv_mid)).astype(jnp.bfloat16)
    second_padded = jnp.where(inside[:, 1:-1], second_padded, jnp.zeros_like(second_padded))
    final_linear_response = feature_conv(second_padded, conv_out)
    latent_layer_three = (
        first_hidden.astype(jnp.float32) + jax.nn.gelu(final_linear_response)
    ).astype(jnp.bfloat16)
    final_layer_result = jnp.einsum(
        "mrwc,cv->mrvw", latent_layer_three, head_weight, preferred_element_type=jnp.float32
    )
    sample_prediction = (
        final_layer_result
        + upsampled_coarse.astype(jnp.float32)[None]
        + per_quantity_offset[None, None, :, None]
    ).astype(jnp.bfloat16)
    row_global = band_row[0] + tile_at * row_count + jnp.arange(row_count, dtype=jnp.int32)
    latitude = math.pi * (row_global.astype(jnp.float32) + 0.5) / GRID_ROWS - math.pi / 2
    row_factor = (jnp.cos(latitude) / (band_rows * col_count))[None, :, None, None]
    var_share = var_count // lax.axis_size("member")
    var_start = lax.axis_index("member") * var_share
    collected_members = lax.all_to_all(
        sample_prediction, "member", split_axis=2, concat_axis=0, tiled=True
    )
    sample_group_predictions = collected_members.astype(jnp.float32)
    member_count = sample_group_predictions.shape[0]
    truth = lax.dynamic_slice_in_dim(target, var_start, var_share, 1).astype(jnp.float32)
    pair_differ = sample_group_predictions[:, None] - sample_group_predictions[None, :]
    abs_sums = jnp.sum(jnp.abs(pair_differ), axis=1)
    sign_sums = jnp.sum(jnp.sign(pair_differ), axis=1)
    crps_map = jnp.mean(jnp.abs(sample_group_predictions - truth[None]), axis=0) - jnp.sum(
        abs_sums, axis=0
    ) / (2 * member_count * (member_count - 1))
    cot_share = (
        row_factor
        * (
            jnp.sign(sample_group_predictions - truth[None]) / member_count
            - sign_sums / (member_count * (member_count - 1))
        )
    ).astype(jnp.bfloat16)
    cotangent = lax.all_to_all(cot_share, "member", split_axis=0, concat_axis=2, tiled=True)
    head_grad = jnp.einsum(
        "mrwc,mrvw->cv", latent_layer_three, cotangent, preferred_element_type=jnp.float32
    )
    bias_grad = jnp.sum(cotangent.astype(jnp.float32), axis=(0, 1, 3))
    back = jnp.einsum("mrvw,cv->mrwc", cotangent, head_weight, preferred_element_type=jnp.float32)
    unused_out, pullback = jax.vjp(jax.nn.gelu, final_linear_response)
    d_pre = pullback(back)[0].astype(jnp.bfloat16)
    second_wide = jnp.pad(second_padded, ((0, 0), (0, 0), (1, 1), (0, 0)))
    rows_of = []
    for i in range(3):
        cols_of = []
        for j in range(3):
            cols_of.append(
                jnp.einsum(
                    "mrwc,mrwd->cd",
                    second_wide[:, i : i + row_count, j : j + col_count],
                    d_pre,
                    preferred_element_type=jnp.float32,
                )
            )
        rows_of.append(jnp.stack(cols_of))
    conv_grad = jnp.stack(rows_of)
    conv_grad, head_grad_t, bias_grad = all_reduce_sum((conv_grad, head_grad.T, bias_grad), ("member", "tile"))
    head_grad = head_grad_t.T
    return (crps_map, conv_grad, head_grad, bias_grad)


def solution(mesh):
    return jax.shard_map(
        on_device,
        mesh=mesh,
        in_specs=(
            P("tile", None, None),
            P("tile", None, None),
            P("member"),
            P(),
            P(),
            P(),
            P(),
            P(),
            P(),
            P(),
            P(),
        ),
        out_specs=(P("tile", "member", None), P(), P(), P()),
        check_vma=False,
    )
```

```python
import math

import jax
import jax.numpy as jnp
from jax import lax
from jax.sharding import Mesh, PartitionSpec as P

GRID_ROWS = 2048
MEMBER = ("group", "core")


def extended(x, sides, width):
    for axis, dim in sides:
        devices, length = (lax.axis_size(axis), x.shape[dim])
        up = [(i, (i + 1) % devices) for i in range(devices - 1)]
        down = [(j, i) for i, j in up]
        last = lax.slice_in_dim(x, length - width, length, axis=dim)
        first = lax.slice_in_dim(x, 0, width, axis=dim)
        before = lax.ppermute(last, axis, up)
        after = lax.ppermute(first, axis, down)
        x = jnp.concatenate([before, x, after], axis=dim)
    return x


def input_conv(padded, kernel):
    out_rows = padded.shape[0] - 2
    col_count = padded.shape[2]
    wide = jnp.pad(padded, ((0, 0), (0, 0), (1, 1)))
    summed = jnp.zeros((out_rows, col_count, kernel.shape[3]), jnp.float32)
    for i in range(3):
        for j in range(3):
            summed = summed + jnp.einsum(
                "rkw,kc->rwc",
                wide[i : i + out_rows, :, j : j + col_count],
                kernel[i, j],
                preferred_element_type=jnp.float32,
            )
    return summed


def feature_conv(padded, kernel):
    out_rows = padded.shape[1] - 2
    col_count = padded.shape[2]
    wide = jnp.pad(padded, ((0, 0), (0, 0), (1, 1), (0, 0)))
    summed = jnp.zeros((padded.shape[0], out_rows, col_count, kernel.shape[3]), jnp.float32)
    for i in range(3):
        for j in range(3):
            summed = summed + jnp.einsum(
                "mrwc,cd->mrwd",
                wide[:, i : i + out_rows, j : j + col_count],
                kernel[i, j],
                preferred_element_type=jnp.float32,
            )
    return summed


def condition(base, cond_scale, cond_shift):
    average = jnp.mean(base, axis=-1, keepdims=True)
    centred = base - average
    spread = jnp.mean(centred * centred, axis=-1, keepdims=True)
    normed = centred * lax.rsqrt(spread + 1e-05)
    mixed = normed[None] * (1.0 + cond_scale[:, None, None, :]) + cond_shift[:, None, None, :]
    return jax.nn.gelu(mixed).astype(jnp.bfloat16)


def abs_terms(probe, sample_group_predictions):

    def abs_single(member_index):
        return jnp.sum(jnp.abs(member_index[None] - sample_group_predictions), axis=0)

    return lax.map(abs_single, probe)


def sign_terms(probe, sample_group_predictions):

    def sign_single(member_index):
        return jnp.sum(jnp.sign(member_index[None] - sample_group_predictions), axis=0)

    return lax.map(sign_single, probe)


def all_reduce_sum(parts):
    peers = ("group", "tile")
    devices = lax.axis_size("group") * lax.axis_size("tile")
    flat = jnp.concatenate([p.reshape(-1) for p in parts])
    total = flat.shape[0]
    width = -(-total // (2 * devices * 128)) * 128
    flat = jnp.pad(flat, (0, 2 * width * devices - total)).reshape(2, devices * width)
    core = lax.axis_index("core")
    swap = [(0, 1), (1, 0)]
    first = core == 0
    keep = jnp.where(first, flat[0], flat[1])
    half = keep + lax.ppermute(jnp.where(first, flat[1], flat[0]), "core", swap)
    pieces = lax.all_to_all(half.reshape(devices, width), peers, 0, 0, tiled=True)
    own = jnp.sum(pieces, axis=0, keepdims=True)
    summed = lax.all_to_all(jnp.broadcast_to(own, (devices, width)), peers, 0, 0, tiled=True)
    summed = summed.reshape(-1)
    other = lax.ppermute(summed, "core", swap)
    spread = jnp.where(first, jnp.concatenate([summed, other]), jnp.concatenate([other, summed]))
    out, at = [], 0
    for p in parts:
        out.append(spread[at : at + p.size].reshape(p.shape))
        at += p.size
    return tuple(out)


def on_device(
    upsampled_coarse,
    target,
    seeds,
    band_row,
    noise_bank,
    cond_weight,
    conv_in,
    conv_mid,
    conv_out,
    head_weight,
    per_quantity_offset,
):
    channels = conv_mid.shape[3]
    row_count = upsampled_coarse.shape[0]
    var_count = upsampled_coarse.shape[1]
    col_count = upsampled_coarse.shape[2]
    tile_count = lax.axis_size("tile")
    tile_at = lax.axis_index("tile")
    band_rows = row_count * tile_count
    selector = (seeds[:, None] == jnp.arange(noise_bank.shape[0], dtype=jnp.int32)[None]).astype(
        jnp.float32
    )
    noise_vec = jnp.dot(selector, noise_bank, precision=lax.Precision.HIGHEST)
    random_latent_gain = jnp.dot(noise_vec, cond_weight, precision=lax.Precision.HIGHEST)
    cond_scale = random_latent_gain[:, :channels]
    cond_shift = random_latent_gain[:, channels:]
    input_padded = extended(upsampled_coarse, (("tile", 0),), 3)
    band_at = tile_at * row_count + jnp.arange(-2, row_count + 2, dtype=jnp.int32)
    inside = ((band_at >= 0) & (band_at < band_rows))[None, :, None, None]
    first_wide = condition(input_conv(input_padded, conv_in), cond_scale, cond_shift)
    first_wide = jnp.where(inside, first_wide, jnp.zeros_like(first_wide))
    first_hidden = first_wide[:, 2 : 2 + row_count]
    second_padded = jax.nn.gelu(feature_conv(first_wide, conv_mid)).astype(jnp.bfloat16)
    second_padded = jnp.where(inside[:, 1:-1], second_padded, jnp.zeros_like(second_padded))
    final_linear_response = feature_conv(second_padded, conv_out)
    latent_layer_three = (
        first_hidden.astype(jnp.float32) + jax.nn.gelu(final_linear_response)
    ).astype(jnp.bfloat16)
    final_layer_result = jnp.einsum(
        "mrwc,cv->mrvw", latent_layer_three, head_weight, preferred_element_type=jnp.float32
    )
    sample_prediction = (
        final_layer_result
        + upsampled_coarse.astype(jnp.float32)[None]
        + per_quantity_offset[None, None, :, None]
    ).astype(jnp.bfloat16)
    row_global = band_row[0] + tile_at * row_count + jnp.arange(row_count, dtype=jnp.int32)
    latitude = math.pi * (row_global.astype(jnp.float32) + 0.5) / GRID_ROWS - math.pi / 2
    row_factor = (jnp.cos(latitude) / (band_rows * col_count))[None, :, None, None]
    var_share = var_count // (lax.axis_size("group") * lax.axis_size("core"))
    var_start = lax.axis_index(MEMBER) * var_share
    collected_members = lax.all_to_all(
        sample_prediction, MEMBER, split_axis=2, concat_axis=0, tiled=True
    )
    sample_group_predictions = collected_members.astype(jnp.float32)
    member_count = sample_group_predictions.shape[0]
    truth = lax.dynamic_slice_in_dim(target, var_start, var_share, 1).astype(jnp.float32)
    pair_differ = sample_group_predictions[:, None] - sample_group_predictions[None, :]
    abs_sums = jnp.sum(jnp.abs(pair_differ), axis=1)
    sign_sums = jnp.sum(jnp.sign(pair_differ), axis=1)
    crps_map = jnp.mean(jnp.abs(sample_group_predictions - truth[None]), axis=0) - jnp.sum(
        abs_sums, axis=0
    ) / (2 * member_count * (member_count - 1))
    cot_share = (
        row_factor
        * (
            jnp.sign(sample_group_predictions - truth[None]) / member_count
            - sign_sums / (member_count * (member_count - 1))
        )
    ).astype(jnp.bfloat16)
    cotangent = lax.all_to_all(cot_share, MEMBER, split_axis=0, concat_axis=2, tiled=True)
    head_grad = jnp.einsum(
        "mrwc,mrvw->cv", latent_layer_three, cotangent, preferred_element_type=jnp.float32
    )
    bias_grad = jnp.sum(cotangent.astype(jnp.float32), axis=(0, 1, 3))
    back = jnp.einsum("mrvw,cv->mrwc", cotangent, head_weight, preferred_element_type=jnp.float32)
    unused_out, pullback = jax.vjp(jax.nn.gelu, final_linear_response)
    d_pre = pullback(back)[0].astype(jnp.bfloat16)
    second_wide = jnp.pad(second_padded, ((0, 0), (0, 0), (1, 1), (0, 0)))
    rows_of = []
    for i in range(3):
        cols_of = []
        for j in range(3):
            cols_of.append(
                jnp.einsum(
                    "mrwc,mrwd->cd",
                    second_wide[:, i : i + row_count, j : j + col_count],
                    d_pre,
                    preferred_element_type=jnp.float32,
                )
            )
        rows_of.append(jnp.stack(cols_of))
    conv_grad = jnp.stack(rows_of)
    conv_grad, head_grad_t, bias_grad = all_reduce_sum((conv_grad, head_grad.T, bias_grad))
    head_grad = head_grad_t.T
    return (crps_map, conv_grad, head_grad, bias_grad)


def solution(mesh):
    members = mesh.shape["member"]
    split = Mesh(
        mesh.devices.reshape(members // 2, 2, mesh.shape["tile"]), ("group", "core", "tile")
    )
    return jax.shard_map(
        on_device,
        mesh=split,
        in_specs=(
            P("tile", None, None),
            P("tile", None, None),
            P(MEMBER),
            P(),
            P(),
            P(),
            P(),
            P(),
            P(),
            P(),
            P(),
        ),
        out_specs=(P("tile", MEMBER, None), P(), P(), P()),
        check_vma=False,
    )
```

```python
import math

import jax
import jax.numpy as jnp
from jax import lax
from jax.sharding import Mesh, PartitionSpec as P

GRID_ROWS = 2048
MEMBER = ("group", "core")


def extended(x, sides, width):
    for axis, dim in sides:
        devices, length = (lax.axis_size(axis), x.shape[dim])
        up = [(i, (i + 1) % devices) for i in range(devices - 1)]
        down = [(j, i) for i, j in up]
        last = lax.slice_in_dim(x, length - width, length, axis=dim)
        first = lax.slice_in_dim(x, 0, width, axis=dim)
        before = lax.ppermute(last, axis, up)
        after = lax.ppermute(first, axis, down)
        x = jnp.concatenate([before, x, after], axis=dim)
    return x


def input_conv(padded, kernel):
    out_rows = padded.shape[0] - 2
    col_count = padded.shape[2]
    wide = jnp.pad(padded, ((0, 0), (0, 0), (1, 1)))
    summed = jnp.zeros((out_rows, col_count, kernel.shape[3]), jnp.float32)
    for i in range(3):
        for j in range(3):
            summed = summed + jnp.einsum(
                "rkw,kc->rwc",
                wide[i : i + out_rows, :, j : j + col_count],
                kernel[i, j],
                preferred_element_type=jnp.float32,
            )
    return summed


def feature_conv(padded, kernel):
    out_rows = padded.shape[1] - 2
    col_count = padded.shape[2]
    wide = jnp.pad(padded, ((0, 0), (0, 0), (1, 1), (0, 0)))
    summed = jnp.zeros((padded.shape[0], out_rows, col_count, kernel.shape[3]), jnp.float32)
    for i in range(3):
        for j in range(3):
            summed = summed + jnp.einsum(
                "mrwc,cd->mrwd",
                wide[:, i : i + out_rows, j : j + col_count],
                kernel[i, j],
                preferred_element_type=jnp.float32,
            )
    return summed


def condition(base, cond_scale, cond_shift):
    average = jnp.mean(base, axis=-1, keepdims=True)
    centred = base - average
    spread = jnp.mean(centred * centred, axis=-1, keepdims=True)
    normed = centred * lax.rsqrt(spread + 1e-05)
    mixed = normed[None] * (1.0 + cond_scale[:, None, None, :]) + cond_shift[:, None, None, :]
    return jax.nn.gelu(mixed).astype(jnp.bfloat16)


def abs_terms(probe, sample_group_predictions):

    def abs_single(member_index):
        return jnp.sum(jnp.abs(member_index[None] - sample_group_predictions), axis=0)

    return lax.map(abs_single, probe)


def sign_terms(probe, sample_group_predictions):

    def sign_single(member_index):
        return jnp.sum(jnp.sign(member_index[None] - sample_group_predictions), axis=0)

    return lax.map(sign_single, probe)


def all_reduce_sum(parts):
    peers = ("group", "tile")
    devices = lax.axis_size("group") * lax.axis_size("tile")
    flat = jnp.concatenate([p.reshape(-1) for p in parts])
    total = flat.shape[0]
    width = -(-total // (2 * devices * 128)) * 128
    flat = jnp.pad(flat, (0, 2 * width * devices - total)).reshape(2, devices * width)
    core = lax.axis_index("core")
    swap = [(0, 1), (1, 0)]
    first = core == 0
    keep = jnp.where(first, flat[0], flat[1])
    half = keep + lax.ppermute(jnp.where(first, flat[1], flat[0]), "core", swap)
    pieces = lax.all_to_all(half.reshape(devices, width), peers, 0, 0, tiled=True)
    own = jnp.sum(pieces, axis=0, keepdims=True)
    summed = lax.all_to_all(jnp.broadcast_to(own, (devices, width)), peers, 0, 0, tiled=True)
    summed = summed.reshape(-1)
    other = lax.ppermute(summed, "core", swap)
    spread = jnp.where(first, jnp.concatenate([summed, other]), jnp.concatenate([other, summed]))
    out, at = [], 0
    for p in parts:
        out.append(spread[at : at + p.size].reshape(p.shape))
        at += p.size
    return tuple(out)


def member_scatter(x, var_share):
    devices = lax.axis_size("group") * lax.axis_size("core")
    rolled = jnp.roll(x, -lax.axis_index(MEMBER) * var_share, axis=2)
    blocks = []
    for k in range(devices):
        block = rolled[:, :, k * var_share : (k + 1) * var_share]
        if k:
            block = lax.ppermute(block, MEMBER, [(s, (s + k) % devices) for s in range(devices)])
        blocks.append(block)
    return jnp.concatenate(blocks, axis=0)


def member_gather(c, var_share, members):
    devices = lax.axis_size("group") * lax.axis_size("core")
    blocks = []
    for k in range(devices):
        block = c[k * members : (k + 1) * members]
        if k:
            block = lax.ppermute(block, MEMBER, [(d, (d - k) % devices) for d in range(devices)])
        blocks.append(block)
    return jnp.roll(jnp.concatenate(blocks, axis=2), lax.axis_index(MEMBER) * var_share, axis=2)


def on_device(
    upsampled_coarse,
    target,
    seeds,
    band_row,
    noise_bank,
    cond_weight,
    conv_in,
    conv_mid,
    conv_out,
    head_weight,
    per_quantity_offset,
):
    channels = conv_mid.shape[3]
    row_count = upsampled_coarse.shape[0]
    var_count = upsampled_coarse.shape[1]
    col_count = upsampled_coarse.shape[2]
    tile_count = lax.axis_size("tile")
    tile_at = lax.axis_index("tile")
    band_rows = row_count * tile_count
    selector = (seeds[:, None] == jnp.arange(noise_bank.shape[0], dtype=jnp.int32)[None]).astype(
        jnp.float32
    )
    noise_vec = jnp.dot(selector, noise_bank, precision=lax.Precision.HIGHEST)
    random_latent_gain = jnp.dot(noise_vec, cond_weight, precision=lax.Precision.HIGHEST)
    cond_scale = random_latent_gain[:, :channels]
    cond_shift = random_latent_gain[:, channels:]
    input_padded = extended(upsampled_coarse, (("tile", 0),), 3)
    band_at = tile_at * row_count + jnp.arange(-2, row_count + 2, dtype=jnp.int32)
    inside = ((band_at >= 0) & (band_at < band_rows))[None, :, None, None]
    first_wide = condition(input_conv(input_padded, conv_in), cond_scale, cond_shift)
    first_wide = jnp.where(inside, first_wide, jnp.zeros_like(first_wide))
    first_hidden = first_wide[:, 2 : 2 + row_count]
    second_padded = jax.nn.gelu(feature_conv(first_wide, conv_mid)).astype(jnp.bfloat16)
    second_padded = jnp.where(inside[:, 1:-1], second_padded, jnp.zeros_like(second_padded))
    final_linear_response = feature_conv(second_padded, conv_out)
    latent_layer_three = (
        first_hidden.astype(jnp.float32) + jax.nn.gelu(final_linear_response)
    ).astype(jnp.bfloat16)
    final_layer_result = jnp.einsum(
        "mrwc,cv->mrvw", latent_layer_three, head_weight, preferred_element_type=jnp.float32
    )
    sample_prediction = (
        final_layer_result
        + upsampled_coarse.astype(jnp.float32)[None]
        + per_quantity_offset[None, None, :, None]
    ).astype(jnp.bfloat16)
    row_global = band_row[0] + tile_at * row_count + jnp.arange(row_count, dtype=jnp.int32)
    latitude = math.pi * (row_global.astype(jnp.float32) + 0.5) / GRID_ROWS - math.pi / 2
    row_factor = (jnp.cos(latitude) / (band_rows * col_count))[None, :, None, None]
    var_share = var_count // (lax.axis_size("group") * lax.axis_size("core"))
    var_start = lax.axis_index(MEMBER) * var_share
    collected_members = member_scatter(sample_prediction, var_share)
    sample_group_predictions = collected_members.astype(jnp.float32)
    member_count = sample_group_predictions.shape[0]
    truth = lax.dynamic_slice_in_dim(target, var_start, var_share, 1).astype(jnp.float32)
    pair_differ = sample_group_predictions[:, None] - sample_group_predictions[None, :]
    abs_sums = jnp.sum(jnp.abs(pair_differ), axis=1)
    sign_sums = jnp.sum(jnp.sign(pair_differ), axis=1)
    crps_map = jnp.mean(jnp.abs(sample_group_predictions - truth[None]), axis=0) - jnp.sum(
        abs_sums, axis=0
    ) / (2 * member_count * (member_count - 1))
    cot_share = (
        row_factor
        * (
            jnp.sign(sample_group_predictions - truth[None]) / member_count
            - sign_sums / (member_count * (member_count - 1))
        )
    ).astype(jnp.bfloat16)
    cotangent = member_gather(cot_share, var_share, sample_prediction.shape[0])
    head_grad = jnp.einsum(
        "mrwc,mrvw->cv", latent_layer_three, cotangent, preferred_element_type=jnp.float32
    )
    bias_grad = jnp.sum(cotangent.astype(jnp.float32), axis=(0, 1, 3))
    back = jnp.einsum("mrvw,cv->mrwc", cotangent, head_weight, preferred_element_type=jnp.float32)
    unused_out, pullback = jax.vjp(jax.nn.gelu, final_linear_response)
    d_pre = pullback(back)[0].astype(jnp.bfloat16)
    second_wide = jnp.pad(second_padded, ((0, 0), (0, 0), (1, 1), (0, 0)))
    rows_of = []
    for i in range(3):
        cols_of = []
        for j in range(3):
            cols_of.append(
                jnp.einsum(
                    "mrwc,mrwd->cd",
                    second_wide[:, i : i + row_count, j : j + col_count],
                    d_pre,
                    preferred_element_type=jnp.float32,
                )
            )
        rows_of.append(jnp.stack(cols_of))
    conv_grad = jnp.stack(rows_of)
    conv_grad, head_grad_t, bias_grad = all_reduce_sum((conv_grad, head_grad.T, bias_grad))
    head_grad = head_grad_t.T
    return (crps_map, conv_grad, head_grad, bias_grad)


def solution(mesh):
    members = mesh.shape["member"]
    split = Mesh(
        mesh.devices.reshape(members // 2, 2, mesh.shape["tile"]), ("group", "core", "tile")
    )
    return jax.shard_map(
        on_device,
        mesh=split,
        in_specs=(
            P("tile", None, None),
            P("tile", None, None),
            P(MEMBER),
            P(),
            P(),
            P(),
            P(),
            P(),
            P(),
            P(),
            P(),
        ),
        out_specs=(P("tile", MEMBER, None), P(), P(), P()),
        check_vma=False,
    )
```

```python
import math

import jax
import jax.numpy as jnp
from jax import lax
from jax.sharding import Mesh, PartitionSpec as P

GRID_ROWS = 2048
MEMBER = ("group", "core")


def extended(x, sides, width):
    for axis, dim in sides:
        devices, length = (lax.axis_size(axis), x.shape[dim])
        up = [(i, (i + 1) % devices) for i in range(devices - 1)]
        down = [(j, i) for i, j in up]
        last = lax.slice_in_dim(x, length - width, length, axis=dim)
        first = lax.slice_in_dim(x, 0, width, axis=dim)
        before = lax.ppermute(last, axis, up)
        after = lax.ppermute(first, axis, down)
        x = jnp.concatenate([before, x, after], axis=dim)
    return x


def input_conv(padded, kernel):
    return lax.conv_general_dilated(
        padded[None],
        kernel,
        window_strides=(1, 1),
        padding=((0, 0), (1, 1)),
        dimension_numbers=("NHCW", "HWIO", "NHWC"),
        preferred_element_type=jnp.float32,
    )[0]


def feature_conv(padded, kernel):
    return lax.conv_general_dilated(
        padded,
        kernel,
        window_strides=(1, 1),
        padding=((0, 0), (1, 1)),
        dimension_numbers=("NHWC", "HWIO", "NHWC"),
        preferred_element_type=jnp.float32,
    )


def kernel_grad(padded, d_out):
    grad = lax.conv_general_dilated(
        padded,
        d_out,
        window_strides=(1, 1),
        padding=((0, 0), (1, 1)),
        dimension_numbers=("CHWN", "IHWO", "NHWC"),
        preferred_element_type=jnp.float32,
    )
    return jnp.transpose(grad, (1, 2, 0, 3))


def condition(base, cond_scale, cond_shift):
    average = jnp.mean(base, axis=-1, keepdims=True)
    centred = base - average
    spread = jnp.mean(centred * centred, axis=-1, keepdims=True)
    normed = centred * lax.rsqrt(spread + 1e-05)
    mixed = normed[None] * (1.0 + cond_scale[:, None, None, :]) + cond_shift[:, None, None, :]
    return jax.nn.gelu(mixed).astype(jnp.bfloat16)


def abs_terms(probe, sample_group_predictions):

    def abs_single(member_index):
        return jnp.sum(jnp.abs(member_index[None] - sample_group_predictions), axis=0)

    return lax.map(abs_single, probe)


def sign_terms(probe, sample_group_predictions):

    def sign_single(member_index):
        return jnp.sum(jnp.sign(member_index[None] - sample_group_predictions), axis=0)

    return lax.map(sign_single, probe)


def all_reduce_sum(parts):
    peers = ("group", "tile")
    devices = lax.axis_size("group") * lax.axis_size("tile")
    flat = jnp.concatenate([p.reshape(-1) for p in parts])
    total = flat.shape[0]
    width = -(-total // (2 * devices * 128)) * 128
    flat = jnp.pad(flat, (0, 2 * width * devices - total)).reshape(2, devices * width)
    core = lax.axis_index("core")
    swap = [(0, 1), (1, 0)]
    first = core == 0
    keep = jnp.where(first, flat[0], flat[1])
    half = keep + lax.ppermute(jnp.where(first, flat[1], flat[0]), "core", swap)
    pieces = lax.all_to_all(half.reshape(devices, width), peers, 0, 0, tiled=True)
    own = jnp.sum(pieces, axis=0, keepdims=True)
    summed = lax.all_to_all(jnp.broadcast_to(own, (devices, width)), peers, 0, 0, tiled=True)
    summed = summed.reshape(-1)
    other = lax.ppermute(summed, "core", swap)
    spread = jnp.where(first, jnp.concatenate([summed, other]), jnp.concatenate([other, summed]))
    out, at = [], 0
    for p in parts:
        out.append(spread[at : at + p.size].reshape(p.shape))
        at += p.size
    return tuple(out)


def on_device(
    upsampled_coarse,
    target,
    seeds,
    band_row,
    noise_bank,
    cond_weight,
    conv_in,
    conv_mid,
    conv_out,
    head_weight,
    per_quantity_offset,
):
    channels = conv_mid.shape[3]
    row_count = upsampled_coarse.shape[0]
    var_count = upsampled_coarse.shape[1]
    col_count = upsampled_coarse.shape[2]
    tile_count = lax.axis_size("tile")
    tile_at = lax.axis_index("tile")
    band_rows = row_count * tile_count
    selector = (seeds[:, None] == jnp.arange(noise_bank.shape[0], dtype=jnp.int32)[None]).astype(
        jnp.float32
    )
    noise_vec = jnp.dot(selector, noise_bank, precision=lax.Precision.HIGHEST)
    random_latent_gain = jnp.dot(noise_vec, cond_weight, precision=lax.Precision.HIGHEST)
    cond_scale = random_latent_gain[:, :channels]
    cond_shift = random_latent_gain[:, channels:]
    input_padded = extended(upsampled_coarse, (("tile", 0),), 3)
    band_at = tile_at * row_count + jnp.arange(-2, row_count + 2, dtype=jnp.int32)
    inside = ((band_at >= 0) & (band_at < band_rows))[None, :, None, None]
    first_wide = condition(input_conv(input_padded, conv_in), cond_scale, cond_shift)
    first_wide = jnp.where(inside, first_wide, jnp.zeros_like(first_wide))
    first_hidden = first_wide[:, 2 : 2 + row_count]
    second_padded = jax.nn.gelu(feature_conv(first_wide, conv_mid)).astype(jnp.bfloat16)
    second_padded = jnp.where(inside[:, 1:-1], second_padded, jnp.zeros_like(second_padded))
    final_linear_response = feature_conv(second_padded, conv_out)
    latent_layer_three = (
        first_hidden.astype(jnp.float32) + jax.nn.gelu(final_linear_response)
    ).astype(jnp.bfloat16)
    final_layer_result = jnp.einsum(
        "mrwc,cv->mrvw", latent_layer_three, head_weight, preferred_element_type=jnp.float32
    )
    sample_prediction = (
        final_layer_result
        + upsampled_coarse.astype(jnp.float32)[None]
        + per_quantity_offset[None, None, :, None]
    ).astype(jnp.bfloat16)
    row_global = band_row[0] + tile_at * row_count + jnp.arange(row_count, dtype=jnp.int32)
    latitude = math.pi * (row_global.astype(jnp.float32) + 0.5) / GRID_ROWS - math.pi / 2
    row_factor = (jnp.cos(latitude) / (band_rows * col_count))[None, :, None, None]
    var_share = var_count // (lax.axis_size("group") * lax.axis_size("core"))
    var_start = lax.axis_index(MEMBER) * var_share
    collected_members = lax.all_to_all(
        sample_prediction, MEMBER, split_axis=2, concat_axis=0, tiled=True
    )
    sample_group_predictions = collected_members.astype(jnp.float32)
    member_count = sample_group_predictions.shape[0]
    truth = lax.dynamic_slice_in_dim(target, var_start, var_share, 1).astype(jnp.float32)
    pair_differ = sample_group_predictions[:, None] - sample_group_predictions[None, :]
    abs_sums = jnp.sum(jnp.abs(pair_differ), axis=1)
    sign_sums = jnp.sum(jnp.sign(pair_differ), axis=1)
    crps_map = jnp.mean(jnp.abs(sample_group_predictions - truth[None]), axis=0) - jnp.sum(
        abs_sums, axis=0
    ) / (2 * member_count * (member_count - 1))
    cot_share = (
        row_factor
        * (
            jnp.sign(sample_group_predictions - truth[None]) / member_count
            - sign_sums / (member_count * (member_count - 1))
        )
    ).astype(jnp.bfloat16)
    cotangent = lax.all_to_all(cot_share, MEMBER, split_axis=0, concat_axis=2, tiled=True)
    head_grad = jnp.einsum(
        "mrwc,mrvw->cv", latent_layer_three, cotangent, preferred_element_type=jnp.float32
    )
    bias_grad = jnp.sum(cotangent.astype(jnp.float32), axis=(0, 1, 3))
    back = jnp.einsum("mrvw,cv->mrwc", cotangent, head_weight, preferred_element_type=jnp.float32)
    unused_out, pullback = jax.vjp(jax.nn.gelu, final_linear_response)
    d_pre = pullback(back)[0].astype(jnp.bfloat16)
    conv_grad = kernel_grad(second_padded, d_pre)
    conv_grad, head_grad_t, bias_grad = all_reduce_sum((conv_grad, head_grad.T, bias_grad))
    head_grad = head_grad_t.T
    return (crps_map, conv_grad, head_grad, bias_grad)


def solution(mesh):
    members = mesh.shape["member"]
    split = Mesh(
        mesh.devices.reshape(members // 2, 2, mesh.shape["tile"]), ("group", "core", "tile")
    )
    return jax.shard_map(
        on_device,
        mesh=split,
        in_specs=(
            P("tile", None, None),
            P("tile", None, None),
            P(MEMBER),
            P(),
            P(),
            P(),
            P(),
            P(),
            P(),
            P(),
            P(),
        ),
        out_specs=(P("tile", MEMBER, None), P(), P(), P()),
        check_vma=False,
    )
```

```python
import math

import jax
import jax.numpy as jnp
from jax import lax
from jax.sharding import Mesh, PartitionSpec as P

GRID_ROWS = 2048
MEMBER = ("group", "core")


def extended(x, sides, width):
    for axis, dim in sides:
        devices, length = (lax.axis_size(axis), x.shape[dim])
        up = [(i, (i + 1) % devices) for i in range(devices - 1)]
        down = [(j, i) for i, j in up]
        last = lax.slice_in_dim(x, length - width, length, axis=dim)
        first = lax.slice_in_dim(x, 0, width, axis=dim)
        before = lax.ppermute(last, axis, up)
        after = lax.ppermute(first, axis, down)
        x = jnp.concatenate([before, x, after], axis=dim)
    return x


def input_conv(padded, kernel):
    out_rows = padded.shape[0] - 2
    col_count = padded.shape[2]
    wide = jnp.pad(padded, ((0, 0), (0, 0), (1, 1)))
    shifted = jnp.concatenate([wide[:, :, j : j + col_count] for j in range(3)], axis=1)
    summed = jnp.zeros((out_rows, col_count, kernel.shape[3]), jnp.float32)
    for i in range(3):
        summed = summed + jnp.einsum(
            "rkw,kc->rwc",
            shifted[i : i + out_rows],
            kernel[i].reshape(-1, kernel.shape[3]),
            preferred_element_type=jnp.float32,
        )
    return summed


def feature_conv(padded, kernel):
    out_rows = padded.shape[1] - 2
    col_count = padded.shape[2]
    wide = jnp.pad(padded, ((0, 0), (0, 0), (1, 1), (0, 0)))
    shifted = jnp.concatenate([wide[:, :, j : j + col_count] for j in range(3)], axis=3)
    summed = jnp.zeros((padded.shape[0], out_rows, col_count, kernel.shape[3]), jnp.float32)
    for i in range(3):
        summed = summed + jnp.einsum(
            "mrwc,cd->mrwd",
            shifted[:, i : i + out_rows],
            kernel[i].reshape(-1, kernel.shape[3]),
            preferred_element_type=jnp.float32,
        )
    return summed


def condition(base, cond_scale, cond_shift):
    average = jnp.mean(base, axis=-1, keepdims=True)
    centred = base - average
    spread = jnp.mean(centred * centred, axis=-1, keepdims=True)
    normed = centred * lax.rsqrt(spread + 1e-05)
    mixed = normed[None] * (1.0 + cond_scale[:, None, None, :]) + cond_shift[:, None, None, :]
    return jax.nn.gelu(mixed).astype(jnp.bfloat16)


def abs_terms(probe, sample_group_predictions):

    def abs_single(member_index):
        return jnp.sum(jnp.abs(member_index[None] - sample_group_predictions), axis=0)

    return lax.map(abs_single, probe)


def sign_terms(probe, sample_group_predictions):

    def sign_single(member_index):
        return jnp.sum(jnp.sign(member_index[None] - sample_group_predictions), axis=0)

    return lax.map(sign_single, probe)


def all_reduce_sum(parts):
    peers = ("group", "tile")
    devices = lax.axis_size("group") * lax.axis_size("tile")
    flat = jnp.concatenate([p.reshape(-1) for p in parts])
    total = flat.shape[0]
    width = -(-total // (2 * devices * 128)) * 128
    flat = jnp.pad(flat, (0, 2 * width * devices - total)).reshape(2, devices * width)
    core = lax.axis_index("core")
    swap = [(0, 1), (1, 0)]
    first = core == 0
    keep = jnp.where(first, flat[0], flat[1])
    half = keep + lax.ppermute(jnp.where(first, flat[1], flat[0]), "core", swap)
    pieces = lax.all_to_all(half.reshape(devices, width), peers, 0, 0, tiled=True)
    own = jnp.sum(pieces, axis=0, keepdims=True)
    summed = lax.all_to_all(jnp.broadcast_to(own, (devices, width)), peers, 0, 0, tiled=True)
    summed = summed.reshape(-1)
    other = lax.ppermute(summed, "core", swap)
    spread = jnp.where(first, jnp.concatenate([summed, other]), jnp.concatenate([other, summed]))
    out, at = [], 0
    for p in parts:
        out.append(spread[at : at + p.size].reshape(p.shape))
        at += p.size
    return tuple(out)


def on_device(
    upsampled_coarse,
    target,
    seeds,
    band_row,
    noise_bank,
    cond_weight,
    conv_in,
    conv_mid,
    conv_out,
    head_weight,
    per_quantity_offset,
):
    channels = conv_mid.shape[3]
    row_count = upsampled_coarse.shape[0]
    var_count = upsampled_coarse.shape[1]
    col_count = upsampled_coarse.shape[2]
    tile_count = lax.axis_size("tile")
    tile_at = lax.axis_index("tile")
    band_rows = row_count * tile_count
    selector = (seeds[:, None] == jnp.arange(noise_bank.shape[0], dtype=jnp.int32)[None]).astype(
        jnp.float32
    )
    noise_vec = jnp.dot(selector, noise_bank, precision=lax.Precision.HIGHEST)
    random_latent_gain = jnp.dot(noise_vec, cond_weight, precision=lax.Precision.HIGHEST)
    cond_scale = random_latent_gain[:, :channels]
    cond_shift = random_latent_gain[:, channels:]
    input_padded = extended(upsampled_coarse, (("tile", 0),), 3)
    band_at = tile_at * row_count + jnp.arange(-2, row_count + 2, dtype=jnp.int32)
    inside = ((band_at >= 0) & (band_at < band_rows))[None, :, None, None]
    first_wide = condition(input_conv(input_padded, conv_in), cond_scale, cond_shift)
    first_wide = jnp.where(inside, first_wide, jnp.zeros_like(first_wide))
    first_hidden = first_wide[:, 2 : 2 + row_count]
    second_padded = jax.nn.gelu(feature_conv(first_wide, conv_mid)).astype(jnp.bfloat16)
    second_padded = jnp.where(inside[:, 1:-1], second_padded, jnp.zeros_like(second_padded))
    final_linear_response = feature_conv(second_padded, conv_out)
    latent_layer_three = (
        first_hidden.astype(jnp.float32) + jax.nn.gelu(final_linear_response)
    ).astype(jnp.bfloat16)
    final_layer_result = jnp.einsum(
        "mrwc,cv->mrvw", latent_layer_three, head_weight, preferred_element_type=jnp.float32
    )
    sample_prediction = (
        final_layer_result
        + upsampled_coarse.astype(jnp.float32)[None]
        + per_quantity_offset[None, None, :, None]
    ).astype(jnp.bfloat16)
    row_global = band_row[0] + tile_at * row_count + jnp.arange(row_count, dtype=jnp.int32)
    latitude = math.pi * (row_global.astype(jnp.float32) + 0.5) / GRID_ROWS - math.pi / 2
    row_factor = (jnp.cos(latitude) / (band_rows * col_count))[None, :, None, None]
    var_share = var_count // (lax.axis_size("group") * lax.axis_size("core"))
    var_start = lax.axis_index(MEMBER) * var_share
    collected_members = lax.all_to_all(
        sample_prediction, MEMBER, split_axis=2, concat_axis=0, tiled=True
    )
    sample_group_predictions = collected_members.astype(jnp.float32)
    member_count = sample_group_predictions.shape[0]
    truth = lax.dynamic_slice_in_dim(target, var_start, var_share, 1).astype(jnp.float32)
    pair_differ = sample_group_predictions[:, None] - sample_group_predictions[None, :]
    abs_sums = jnp.sum(jnp.abs(pair_differ), axis=1)
    sign_sums = jnp.sum(jnp.sign(pair_differ), axis=1)
    crps_map = jnp.mean(jnp.abs(sample_group_predictions - truth[None]), axis=0) - jnp.sum(
        abs_sums, axis=0
    ) / (2 * member_count * (member_count - 1))
    cot_share = (
        row_factor
        * (
            jnp.sign(sample_group_predictions - truth[None]) / member_count
            - sign_sums / (member_count * (member_count - 1))
        )
    ).astype(jnp.bfloat16)
    cotangent = lax.all_to_all(cot_share, MEMBER, split_axis=0, concat_axis=2, tiled=True)
    head_grad = jnp.einsum(
        "mrwc,mrvw->cv", latent_layer_three, cotangent, preferred_element_type=jnp.float32
    )
    bias_grad = jnp.sum(cotangent.astype(jnp.float32), axis=(0, 1, 3))
    back = jnp.einsum("mrvw,cv->mrwc", cotangent, head_weight, preferred_element_type=jnp.float32)
    unused_out, pullback = jax.vjp(jax.nn.gelu, final_linear_response)
    d_pre = pullback(back)[0].astype(jnp.bfloat16)
    second_wide = jnp.pad(second_padded, ((0, 0), (0, 0), (1, 1), (0, 0)))
    rows_of = []
    for i in range(3):
        cols_of = []
        for j in range(3):
            cols_of.append(
                jnp.einsum(
                    "mrwc,mrwd->cd",
                    second_wide[:, i : i + row_count, j : j + col_count],
                    d_pre,
                    preferred_element_type=jnp.float32,
                )
            )
        rows_of.append(jnp.stack(cols_of))
    conv_grad = jnp.stack(rows_of)
    conv_grad, head_grad_t, bias_grad = all_reduce_sum((conv_grad, head_grad.T, bias_grad))
    head_grad = head_grad_t.T
    return (crps_map, conv_grad, head_grad, bias_grad)


def solution(mesh):
    members = mesh.shape["member"]
    split = Mesh(
        mesh.devices.reshape(members // 2, 2, mesh.shape["tile"]), ("group", "core", "tile")
    )
    return jax.shard_map(
        on_device,
        mesh=split,
        in_specs=(
            P("tile", None, None),
            P("tile", None, None),
            P(MEMBER),
            P(),
            P(),
            P(),
            P(),
            P(),
            P(),
            P(),
            P(),
        ),
        out_specs=(P("tile", MEMBER, None), P(), P(), P()),
        check_vma=False,
    )
```

```python
import math

import jax
import jax.numpy as jnp
from jax import lax
from jax.sharding import Mesh, PartitionSpec as P

GRID_ROWS = 2048
MEMBER = ("group", "core")


def extended(x, sides, width):
    for axis, dim in sides:
        devices, length = (lax.axis_size(axis), x.shape[dim])
        up = [(i, (i + 1) % devices) for i in range(devices - 1)]
        down = [(j, i) for i, j in up]
        last = lax.slice_in_dim(x, length - width, length, axis=dim)
        first = lax.slice_in_dim(x, 0, width, axis=dim)
        before = lax.ppermute(last, axis, up)
        after = lax.ppermute(first, axis, down)
        x = jnp.concatenate([before, x, after], axis=dim)
    return x


def input_conv(padded, kernel):
    out_rows = padded.shape[0] - 2
    col_count = padded.shape[2]
    wide = jnp.pad(padded, ((0, 0), (0, 0), (1, 1)))
    shifted = jnp.concatenate([wide[:, :, j : j + col_count] for j in range(3)], axis=1)
    summed = jnp.zeros((out_rows, col_count, kernel.shape[3]), jnp.float32)
    for i in range(3):
        summed = summed + jnp.einsum(
            "rkw,kc->rwc",
            shifted[i : i + out_rows],
            kernel[i].reshape(-1, kernel.shape[3]),
            preferred_element_type=jnp.float32,
        )
    return summed


def feature_conv(padded, kernel):
    out_rows = padded.shape[1] - 2
    col_count = padded.shape[2]
    wide = jnp.pad(padded, ((0, 0), (0, 0), (1, 1), (0, 0)))
    shifted = jnp.concatenate([wide[:, :, j : j + col_count] for j in range(3)], axis=3)
    summed = jnp.zeros((padded.shape[0], out_rows, col_count, kernel.shape[3]), jnp.float32)
    for i in range(3):
        summed = summed + jnp.einsum(
            "mrwc,cd->mrwd",
            shifted[:, i : i + out_rows],
            kernel[i].reshape(-1, kernel.shape[3]),
            preferred_element_type=jnp.float32,
        )
    return summed


def condition(base, cond_scale, cond_shift):
    average = jnp.mean(base, axis=-1, keepdims=True)
    centred = base - average
    spread = jnp.mean(centred * centred, axis=-1, keepdims=True)
    normed = centred * lax.rsqrt(spread + 1e-05)
    mixed = normed[None] * (1.0 + cond_scale[:, None, None, :]) + cond_shift[:, None, None, :]
    return jax.nn.gelu(mixed).astype(jnp.bfloat16)


def abs_terms(probe, sample_group_predictions):

    def abs_single(member_index):
        return jnp.sum(jnp.abs(member_index[None] - sample_group_predictions), axis=0)

    return lax.map(abs_single, probe)


def sign_terms(probe, sample_group_predictions):

    def sign_single(member_index):
        return jnp.sum(jnp.sign(member_index[None] - sample_group_predictions), axis=0)

    return lax.map(sign_single, probe)


def all_reduce_sum(parts):
    peers = ("group", "tile")
    devices = lax.axis_size("group") * lax.axis_size("tile")
    flat = jnp.concatenate([p.reshape(-1) for p in parts])
    total = flat.shape[0]
    width = -(-total // (2 * devices * 128)) * 128
    flat = jnp.pad(flat, (0, 2 * width * devices - total)).reshape(2, devices * width)
    core = lax.axis_index("core")
    swap = [(0, 1), (1, 0)]
    first = core == 0
    keep = jnp.where(first, flat[0], flat[1])
    half = keep + lax.ppermute(jnp.where(first, flat[1], flat[0]), "core", swap)
    pieces = lax.all_to_all(half.reshape(devices, width), peers, 0, 0, tiled=True)
    own = jnp.sum(pieces, axis=0, keepdims=True)
    summed = lax.all_to_all(jnp.broadcast_to(own, (devices, width)), peers, 0, 0, tiled=True)
    summed = summed.reshape(-1)
    other = lax.ppermute(summed, "core", swap)
    spread = jnp.where(first, jnp.concatenate([summed, other]), jnp.concatenate([other, summed]))
    out, at = [], 0
    for p in parts:
        out.append(spread[at : at + p.size].reshape(p.shape))
        at += p.size
    return tuple(out)


def on_device(
    upsampled_coarse,
    target,
    seeds,
    band_row,
    noise_bank,
    cond_weight,
    conv_in,
    conv_mid,
    conv_out,
    head_weight,
    per_quantity_offset,
):
    channels = conv_mid.shape[3]
    row_count = upsampled_coarse.shape[0]
    var_count = upsampled_coarse.shape[1]
    col_count = upsampled_coarse.shape[2]
    tile_count = lax.axis_size("tile")
    tile_at = lax.axis_index("tile")
    band_rows = row_count * tile_count
    selector = (seeds[:, None] == jnp.arange(noise_bank.shape[0], dtype=jnp.int32)[None]).astype(
        jnp.float32
    )
    noise_vec = jnp.dot(selector, noise_bank, precision=lax.Precision.HIGHEST)
    random_latent_gain = jnp.dot(noise_vec, cond_weight, precision=lax.Precision.HIGHEST)
    cond_scale = random_latent_gain[:, :channels]
    cond_shift = random_latent_gain[:, channels:]
    input_padded = extended(upsampled_coarse, (("tile", 0),), 3)
    band_at = tile_at * row_count + jnp.arange(-2, row_count + 2, dtype=jnp.int32)
    inside = ((band_at >= 0) & (band_at < band_rows))[None, :, None, None]
    first_wide = condition(input_conv(input_padded, conv_in), cond_scale, cond_shift)
    first_wide = jnp.where(inside, first_wide, jnp.zeros_like(first_wide))
    first_hidden = first_wide[:, 2 : 2 + row_count]
    second_padded = jax.nn.gelu(feature_conv(first_wide, conv_mid)).astype(jnp.bfloat16)
    second_padded = jnp.where(inside[:, 1:-1], second_padded, jnp.zeros_like(second_padded))
    final_linear_response = feature_conv(second_padded, conv_out)
    latent_layer_three = (
        first_hidden.astype(jnp.float32) + jax.nn.gelu(final_linear_response)
    ).astype(jnp.bfloat16)
    final_layer_result = jnp.einsum(
        "mrwc,cv->mrvw", latent_layer_three, head_weight, preferred_element_type=jnp.float32
    )
    sample_prediction = (
        final_layer_result
        + upsampled_coarse.astype(jnp.float32)[None]
        + per_quantity_offset[None, None, :, None]
    ).astype(jnp.bfloat16)
    row_global = band_row[0] + tile_at * row_count + jnp.arange(row_count, dtype=jnp.int32)
    latitude = math.pi * (row_global.astype(jnp.float32) + 0.5) / GRID_ROWS - math.pi / 2
    row_factor = (jnp.cos(latitude) / (band_rows * col_count))[None, :, None, None]
    var_share = var_count // (lax.axis_size("group") * lax.axis_size("core"))
    var_start = lax.axis_index(MEMBER) * var_share
    collected_members = lax.all_to_all(
        sample_prediction, MEMBER, split_axis=2, concat_axis=0, tiled=True
    )
    sample_group_predictions = collected_members.astype(jnp.float32)
    member_count = sample_group_predictions.shape[0]
    truth = lax.dynamic_slice_in_dim(target, var_start, var_share, 1).astype(jnp.float32)
    pair_differ = sample_group_predictions[:, None] - sample_group_predictions[None, :]
    abs_sums = jnp.sum(jnp.abs(pair_differ), axis=1)
    sign_sums = jnp.sum(jnp.sign(pair_differ), axis=1)
    crps_map = jnp.mean(jnp.abs(sample_group_predictions - truth[None]), axis=0) - jnp.sum(
        abs_sums, axis=0
    ) / (2 * member_count * (member_count - 1))
    cot_share = (
        row_factor
        * (
            jnp.sign(sample_group_predictions - truth[None]) / member_count
            - sign_sums / (member_count * (member_count - 1))
        )
    ).astype(jnp.bfloat16)
    cotangent = lax.all_to_all(cot_share, MEMBER, split_axis=0, concat_axis=2, tiled=True)
    head_grad = jnp.einsum(
        "mrwc,mrvw->cv", latent_layer_three, cotangent, preferred_element_type=jnp.float32
    )
    bias_grad = jnp.sum(cotangent.astype(jnp.float32), axis=(0, 1, 3))
    back = jnp.einsum("mrvw,cv->mrwc", cotangent, head_weight, preferred_element_type=jnp.float32)
    unused_out, pullback = jax.vjp(jax.nn.gelu, final_linear_response)
    d_pre = pullback(back)[0].astype(jnp.bfloat16)
    second_wide = jnp.pad(second_padded, ((0, 0), (0, 0), (1, 1), (0, 0)))
    second_shifted = jnp.concatenate([second_wide[:, :, j : j + col_count] for j in range(3)], axis=3)
    conv_grad = jnp.stack(
        [
            jnp.einsum(
                "mrwk,mrwd->kd",
                second_shifted[:, i : i + row_count],
                d_pre,
                preferred_element_type=jnp.float32,
            ).reshape(conv_out.shape[1:])
            for i in range(3)
        ]
    )
    conv_grad, head_grad_t, bias_grad = all_reduce_sum((conv_grad, head_grad.T, bias_grad))
    head_grad = head_grad_t.T
    return (crps_map, conv_grad, head_grad, bias_grad)


def solution(mesh):
    members = mesh.shape["member"]
    split = Mesh(
        mesh.devices.reshape(members // 2, 2, mesh.shape["tile"]), ("group", "core", "tile")
    )
    return jax.shard_map(
        on_device,
        mesh=split,
        in_specs=(
            P("tile", None, None),
            P("tile", None, None),
            P(MEMBER),
            P(),
            P(),
            P(),
            P(),
            P(),
            P(),
            P(),
            P(),
        ),
        out_specs=(P("tile", MEMBER, None), P(), P(), P()),
        check_vma=False,
    )
```

```python
import math

import jax
import jax.numpy as jnp
from jax import lax
from jax.sharding import Mesh, PartitionSpec as P

GRID_ROWS = 2048
MEMBER = ("group", "core")


def extended(x, sides, width):
    for axis, dim in sides:
        devices, length = (lax.axis_size(axis), x.shape[dim])
        up = [(i, (i + 1) % devices) for i in range(devices - 1)]
        down = [(j, i) for i, j in up]
        last = lax.slice_in_dim(x, length - width, length, axis=dim)
        first = lax.slice_in_dim(x, 0, width, axis=dim)
        before = lax.ppermute(last, axis, up)
        after = lax.ppermute(first, axis, down)
        x = jnp.concatenate([before, x, after], axis=dim)
    return x


def input_conv(padded, kernel):
    out_rows = padded.shape[0] - 2
    col_count = padded.shape[2]
    wide = jnp.pad(padded, ((0, 0), (0, 0), (1, 1)))
    shifted = jnp.concatenate([wide[:, :, j : j + col_count] for j in range(3)], axis=1)
    summed = jnp.zeros((out_rows, col_count, kernel.shape[3]), jnp.float32)
    for i in range(3):
        summed = summed + jnp.einsum(
            "rkw,kc->rwc",
            shifted[i : i + out_rows],
            kernel[i].reshape(-1, kernel.shape[3]),
            preferred_element_type=jnp.float32,
        )
    return summed


def feature_conv(padded, kernel):
    out_rows = padded.shape[1] - 2
    col_count = padded.shape[2]
    wide = jnp.pad(padded, ((0, 0), (0, 0), (1, 1), (0, 0)))
    shifted = jnp.concatenate([wide[:, :, j : j + col_count] for j in range(3)], axis=3)
    summed = jnp.zeros((padded.shape[0], out_rows, col_count, kernel.shape[3]), jnp.float32)
    for i in range(3):
        summed = summed + jnp.einsum(
            "mrwc,cd->mrwd",
            shifted[:, i : i + out_rows],
            kernel[i].reshape(-1, kernel.shape[3]),
            preferred_element_type=jnp.float32,
        )
    return summed


def condition(base, cond_scale, cond_shift):
    average = jnp.mean(base, axis=-1, keepdims=True)
    centred = base - average
    spread = jnp.mean(centred * centred, axis=-1, keepdims=True)
    normed = centred * lax.rsqrt(spread + 1e-05)
    mixed = normed[None] * (1.0 + cond_scale[:, None, None, :]) + cond_shift[:, None, None, :]
    return jax.nn.gelu(mixed).astype(jnp.bfloat16)


def abs_terms(probe, sample_group_predictions):

    def abs_single(member_index):
        return jnp.sum(jnp.abs(member_index[None] - sample_group_predictions), axis=0)

    return lax.map(abs_single, probe)


def sign_terms(probe, sample_group_predictions):

    def sign_single(member_index):
        return jnp.sum(jnp.sign(member_index[None] - sample_group_predictions), axis=0)

    return lax.map(sign_single, probe)


def all_reduce_sum(parts):
    peers = ("group", "tile")
    devices = lax.axis_size("group") * lax.axis_size("tile")
    flat = jnp.concatenate([p.reshape(-1) for p in parts])
    total = flat.shape[0]
    width = -(-total // (2 * devices * 128)) * 128
    flat = jnp.pad(flat, (0, 2 * width * devices - total)).reshape(2, devices * width)
    core = lax.axis_index("core")
    swap = [(0, 1), (1, 0)]
    first = core == 0
    keep = jnp.where(first, flat[0], flat[1])
    half = keep + lax.ppermute(jnp.where(first, flat[1], flat[0]), "core", swap)
    pieces = lax.all_to_all(half.reshape(devices, width), peers, 0, 0, tiled=True)
    own = jnp.sum(pieces, axis=0, keepdims=True)
    summed = lax.all_to_all(jnp.broadcast_to(own, (devices, width)), peers, 0, 0, tiled=True)
    summed = summed.reshape(-1)
    other = lax.ppermute(summed, "core", swap)
    spread = jnp.where(first, jnp.concatenate([summed, other]), jnp.concatenate([other, summed]))
    out, at = [], 0
    for p in parts:
        out.append(spread[at : at + p.size].reshape(p.shape))
        at += p.size
    return tuple(out)


def on_device(
    upsampled_coarse,
    target,
    seeds,
    band_row,
    noise_bank,
    cond_weight,
    conv_in,
    conv_mid,
    conv_out,
    head_weight,
    per_quantity_offset,
):
    channels = conv_mid.shape[3]
    row_count = upsampled_coarse.shape[0]
    var_count = upsampled_coarse.shape[1]
    col_count = upsampled_coarse.shape[2]
    tile_count = lax.axis_size("tile")
    tile_at = lax.axis_index("tile")
    band_rows = row_count * tile_count
    selector = (seeds[:, None] == jnp.arange(noise_bank.shape[0], dtype=jnp.int32)[None]).astype(
        jnp.float32
    )
    noise_vec = jnp.dot(selector, noise_bank, precision=lax.Precision.HIGHEST)
    random_latent_gain = jnp.dot(noise_vec, cond_weight, precision=lax.Precision.HIGHEST)
    cond_scale = random_latent_gain[:, :channels]
    cond_shift = random_latent_gain[:, channels:]
    input_padded = extended(upsampled_coarse, (("tile", 0),), 3)
    band_at = tile_at * row_count + jnp.arange(-2, row_count + 2, dtype=jnp.int32)
    inside = ((band_at >= 0) & (band_at < band_rows))[None, :, None, None]
    first_wide = condition(input_conv(input_padded, conv_in), cond_scale, cond_shift)
    first_wide = jnp.where(inside, first_wide, jnp.zeros_like(first_wide))
    first_hidden = first_wide[:, 2 : 2 + row_count]
    second_padded = jax.nn.gelu(feature_conv(first_wide, conv_mid)).astype(jnp.bfloat16)
    second_padded = jnp.where(inside[:, 1:-1], second_padded, jnp.zeros_like(second_padded))
    final_linear_response = feature_conv(second_padded, conv_out)
    latent_layer_three = (
        first_hidden.astype(jnp.float32) + jax.nn.gelu(final_linear_response)
    ).astype(jnp.bfloat16)
    final_layer_result = jnp.einsum(
        "mrwc,cv->vmrw", latent_layer_three, head_weight, preferred_element_type=jnp.float32
    )
    sample_prediction = (
        final_layer_result
        + jnp.transpose(upsampled_coarse, (1, 0, 2)).astype(jnp.float32)[:, None]
        + per_quantity_offset[:, None, None, None]
    ).astype(jnp.bfloat16)
    row_global = band_row[0] + tile_at * row_count + jnp.arange(row_count, dtype=jnp.int32)
    latitude = math.pi * (row_global.astype(jnp.float32) + 0.5) / GRID_ROWS - math.pi / 2
    row_factor = (jnp.cos(latitude) / (band_rows * col_count))[None, None, :, None]
    var_share = var_count // (lax.axis_size("group") * lax.axis_size("core"))
    var_start = lax.axis_index(MEMBER) * var_share
    collected_members = lax.all_to_all(
        sample_prediction, MEMBER, split_axis=0, concat_axis=1, tiled=True
    )
    sample_group_predictions = collected_members.astype(jnp.float32)
    member_count = sample_group_predictions.shape[1]
    truth = jnp.transpose(
        lax.dynamic_slice_in_dim(target, var_start, var_share, 1), (1, 0, 2)
    ).astype(jnp.float32)[:, None]
    pair_differ = sample_group_predictions[:, :, None] - sample_group_predictions[:, None, :]
    abs_sums = jnp.sum(jnp.abs(pair_differ), axis=2)
    sign_sums = jnp.sum(jnp.sign(pair_differ), axis=2)
    crps_share = jnp.mean(jnp.abs(sample_group_predictions - truth), axis=1) - jnp.sum(
        abs_sums, axis=1
    ) / (2 * member_count * (member_count - 1))
    crps_map = jnp.transpose(crps_share, (1, 0, 2))
    cot_share = (
        row_factor
        * (
            jnp.sign(sample_group_predictions - truth) / member_count
            - sign_sums / (member_count * (member_count - 1))
        )
    ).astype(jnp.bfloat16)
    cotangent = lax.all_to_all(cot_share, MEMBER, split_axis=1, concat_axis=0, tiled=True)
    head_grad = jnp.einsum(
        "mrwc,vmrw->cv", latent_layer_three, cotangent, preferred_element_type=jnp.float32
    )
    bias_grad = jnp.sum(cotangent.astype(jnp.float32), axis=(1, 2, 3))
    back = jnp.einsum("vmrw,cv->mrwc", cotangent, head_weight, preferred_element_type=jnp.float32)
    unused_out, pullback = jax.vjp(jax.nn.gelu, final_linear_response)
    d_pre = pullback(back)[0].astype(jnp.bfloat16)
    second_wide = jnp.pad(second_padded, ((0, 0), (0, 0), (1, 1), (0, 0)))
    rows_of = []
    for i in range(3):
        cols_of = []
        for j in range(3):
            cols_of.append(
                jnp.einsum(
                    "mrwc,mrwd->cd",
                    second_wide[:, i : i + row_count, j : j + col_count],
                    d_pre,
                    preferred_element_type=jnp.float32,
                )
            )
        rows_of.append(jnp.stack(cols_of))
    conv_grad = jnp.stack(rows_of)
    conv_grad, head_grad_t, bias_grad = all_reduce_sum((conv_grad, head_grad.T, bias_grad))
    head_grad = head_grad_t.T
    return (crps_map, conv_grad, head_grad, bias_grad)


def solution(mesh):
    members = mesh.shape["member"]
    split = Mesh(
        mesh.devices.reshape(members // 2, 2, mesh.shape["tile"]), ("group", "core", "tile")
    )
    return jax.shard_map(
        on_device,
        mesh=split,
        in_specs=(
            P("tile", None, None),
            P("tile", None, None),
            P(MEMBER),
            P(),
            P(),
            P(),
            P(),
            P(),
            P(),
            P(),
            P(),
        ),
        out_specs=(P("tile", MEMBER, None), P(), P(), P()),
        check_vma=False,
    )
```

```python
import math

import jax
import jax.numpy as jnp
from jax import lax
from jax.sharding import Mesh, PartitionSpec as P

GRID_ROWS = 2048
MEMBER = ("group", "core")


def extended(x, sides, width):
    for axis, dim in sides:
        devices, length = (lax.axis_size(axis), x.shape[dim])
        up = [(i, (i + 1) % devices) for i in range(devices - 1)]
        down = [(j, i) for i, j in up]
        last = lax.slice_in_dim(x, length - width, length, axis=dim)
        first = lax.slice_in_dim(x, 0, width, axis=dim)
        before = lax.ppermute(last, axis, up)
        after = lax.ppermute(first, axis, down)
        x = jnp.concatenate([before, x, after], axis=dim)
    return x


def input_conv(padded, kernel):
    out_rows = padded.shape[0] - 2
    col_count = padded.shape[2]
    wide = jnp.pad(padded, ((0, 0), (0, 0), (1, 1)))
    shifted = jnp.concatenate([wide[:, :, j : j + col_count] for j in range(3)], axis=1)
    summed = jnp.zeros((out_rows, col_count, kernel.shape[3]), jnp.float32)
    for i in range(3):
        summed = summed + jnp.einsum(
            "rkw,kc->rwc",
            shifted[i : i + out_rows],
            kernel[i].reshape(-1, kernel.shape[3]),
            preferred_element_type=jnp.float32,
        )
    return summed


def feature_conv(padded, kernel):
    out_rows = padded.shape[1] - 2
    col_count = padded.shape[2]
    wide = jnp.pad(padded, ((0, 0), (0, 0), (1, 1), (0, 0)))
    shifted = jnp.concatenate([wide[:, :, j : j + col_count] for j in range(3)], axis=3)
    summed = jnp.zeros((padded.shape[0], out_rows, col_count, kernel.shape[3]), jnp.float32)
    for i in range(3):
        summed = summed + jnp.einsum(
            "mrwc,cd->mrwd",
            shifted[:, i : i + out_rows],
            kernel[i].reshape(-1, kernel.shape[3]),
            preferred_element_type=jnp.float32,
        )
    return summed


def condition(base, cond_scale, cond_shift):
    average = jnp.mean(base, axis=-1, keepdims=True)
    centred = base - average
    spread = jnp.mean(centred * centred, axis=-1, keepdims=True)
    normed = centred * lax.rsqrt(spread + 1e-05)
    mixed = normed[None] * (1.0 + cond_scale[:, None, None, :]) + cond_shift[:, None, None, :]
    return jax.nn.gelu(mixed).astype(jnp.bfloat16)


def abs_terms(probe, sample_group_predictions):

    def abs_single(member_index):
        return jnp.sum(jnp.abs(member_index[None] - sample_group_predictions), axis=0)

    return lax.map(abs_single, probe)


def sign_terms(probe, sample_group_predictions):

    def sign_single(member_index):
        return jnp.sum(jnp.sign(member_index[None] - sample_group_predictions), axis=0)

    return lax.map(sign_single, probe)


def all_reduce_sum(parts):
    peers = ("group", "tile")
    devices = lax.axis_size("group") * lax.axis_size("tile")
    flat = jnp.concatenate([p.reshape(-1) for p in parts])
    total = flat.shape[0]
    width = -(-total // (2 * devices * 128)) * 128
    flat = jnp.pad(flat, (0, 2 * width * devices - total))
    core = lax.axis_index("core")
    swap = [(0, 1), (1, 0)]
    size = width * devices
    keep = lax.dynamic_slice_in_dim(flat, core * size, size)
    send = lax.dynamic_slice_in_dim(flat, (1 - core) * size, size)
    half = keep + lax.ppermute(send, "core", swap)
    pieces = lax.all_to_all(half.reshape(devices, width), peers, 0, 0, tiled=True)
    own = jnp.sum(pieces, axis=0, keepdims=True)
    summed = lax.all_to_all(jnp.broadcast_to(own, (devices, width)), peers, 0, 0, tiled=True)
    summed = summed.reshape(-1)
    other = lax.ppermute(summed, "core", swap)
    spread = lax.dynamic_update_slice_in_dim(jnp.zeros_like(flat), summed, core * size, 0)
    spread = lax.dynamic_update_slice_in_dim(spread, other, (1 - core) * size, 0)
    out, at = [], 0
    for p in parts:
        out.append(spread[at : at + p.size].reshape(p.shape))
        at += p.size
    return tuple(out)


def on_device(
    upsampled_coarse,
    target,
    seeds,
    band_row,
    noise_bank,
    cond_weight,
    conv_in,
    conv_mid,
    conv_out,
    head_weight,
    per_quantity_offset,
):
    channels = conv_mid.shape[3]
    row_count = upsampled_coarse.shape[0]
    var_count = upsampled_coarse.shape[1]
    col_count = upsampled_coarse.shape[2]
    tile_count = lax.axis_size("tile")
    tile_at = lax.axis_index("tile")
    band_rows = row_count * tile_count
    selector = (seeds[:, None] == jnp.arange(noise_bank.shape[0], dtype=jnp.int32)[None]).astype(
        jnp.float32
    )
    noise_vec = jnp.dot(selector, noise_bank, precision=lax.Precision.HIGHEST)
    random_latent_gain = jnp.dot(noise_vec, cond_weight, precision=lax.Precision.HIGHEST)
    cond_scale = random_latent_gain[:, :channels]
    cond_shift = random_latent_gain[:, channels:]
    input_padded = extended(upsampled_coarse, (("tile", 0),), 3)
    band_at = tile_at * row_count + jnp.arange(-2, row_count + 2, dtype=jnp.int32)
    inside = ((band_at >= 0) & (band_at < band_rows))[None, :, None, None]
    first_wide = condition(input_conv(input_padded, conv_in), cond_scale, cond_shift)
    first_wide = jnp.where(inside, first_wide, jnp.zeros_like(first_wide))
    first_hidden = first_wide[:, 2 : 2 + row_count]
    second_padded = jax.nn.gelu(feature_conv(first_wide, conv_mid)).astype(jnp.bfloat16)
    second_padded = jnp.where(inside[:, 1:-1], second_padded, jnp.zeros_like(second_padded))
    final_linear_response = feature_conv(second_padded, conv_out)
    latent_layer_three = (
        first_hidden.astype(jnp.float32) + jax.nn.gelu(final_linear_response)
    ).astype(jnp.bfloat16)
    final_layer_result = jnp.einsum(
        "mrwc,cv->vmrw", latent_layer_three, head_weight, preferred_element_type=jnp.float32
    )
    sample_prediction = (
        final_layer_result
        + jnp.transpose(upsampled_coarse, (1, 0, 2)).astype(jnp.float32)[:, None]
        + per_quantity_offset[:, None, None, None]
    ).astype(jnp.bfloat16)
    row_global = band_row[0] + tile_at * row_count + jnp.arange(row_count, dtype=jnp.int32)
    latitude = math.pi * (row_global.astype(jnp.float32) + 0.5) / GRID_ROWS - math.pi / 2
    row_factor = (jnp.cos(latitude) / (band_rows * col_count))[None, None, :, None]
    var_share = var_count // (lax.axis_size("group") * lax.axis_size("core"))
    var_start = lax.axis_index(MEMBER) * var_share
    collected_members = lax.all_to_all(
        sample_prediction, MEMBER, split_axis=0, concat_axis=1, tiled=True
    )
    sample_group_predictions = collected_members.astype(jnp.float32)
    member_count = sample_group_predictions.shape[1]
    truth = jnp.transpose(
        lax.dynamic_slice_in_dim(target, var_start, var_share, 1), (1, 0, 2)
    ).astype(jnp.float32)[:, None]
    pair_differ = sample_group_predictions[:, :, None] - sample_group_predictions[:, None, :]
    abs_sums = jnp.sum(jnp.abs(pair_differ), axis=2)
    sign_sums = jnp.sum(jnp.sign(pair_differ), axis=2)
    crps_share = jnp.mean(jnp.abs(sample_group_predictions - truth), axis=1) - jnp.sum(
        abs_sums, axis=1
    ) / (2 * member_count * (member_count - 1))
    crps_map = jnp.transpose(crps_share, (1, 0, 2))
    cot_share = (
        row_factor
        * (
            jnp.sign(sample_group_predictions - truth) / member_count
            - sign_sums / (member_count * (member_count - 1))
        )
    ).astype(jnp.bfloat16)
    cotangent = lax.all_to_all(cot_share, MEMBER, split_axis=1, concat_axis=0, tiled=True)
    head_grad = jnp.einsum(
        "mrwc,vmrw->cv", latent_layer_three, cotangent, preferred_element_type=jnp.float32
    )
    bias_grad = jnp.sum(cotangent.astype(jnp.float32), axis=(1, 2, 3))
    back = jnp.einsum("vmrw,cv->mrwc", cotangent, head_weight, preferred_element_type=jnp.float32)
    unused_out, pullback = jax.vjp(jax.nn.gelu, final_linear_response)
    d_pre = pullback(back)[0].astype(jnp.bfloat16)
    second_wide = jnp.pad(second_padded, ((0, 0), (0, 0), (1, 1), (0, 0)))
    rows_of = []
    for i in range(3):
        cols_of = []
        for j in range(3):
            cols_of.append(
                jnp.einsum(
                    "mrwc,mrwd->cd",
                    second_wide[:, i : i + row_count, j : j + col_count],
                    d_pre,
                    preferred_element_type=jnp.float32,
                )
            )
        rows_of.append(jnp.stack(cols_of))
    conv_grad = jnp.stack(rows_of)
    conv_grad, head_grad_t, bias_grad = all_reduce_sum((conv_grad, head_grad.T, bias_grad))
    head_grad = head_grad_t.T
    return (crps_map, conv_grad, head_grad, bias_grad)


def solution(mesh):
    members = mesh.shape["member"]
    split = Mesh(
        mesh.devices.reshape(members // 2, 2, mesh.shape["tile"]), ("group", "core", "tile")
    )
    return jax.shard_map(
        on_device,
        mesh=split,
        in_specs=(
            P("tile", None, None),
            P("tile", None, None),
            P(MEMBER),
            P(),
            P(),
            P(),
            P(),
            P(),
            P(),
            P(),
            P(),
        ),
        out_specs=(P("tile", MEMBER, None), P(), P(), P()),
        check_vma=False,
    )
```

```python
import math

import jax
import jax.numpy as jnp
from jax import lax
from jax.sharding import Mesh, PartitionSpec as P

GRID_ROWS = 2048
MEMBER = ("group", "core")


def extended(x, sides, width):
    for axis, dim in sides:
        devices, length = (lax.axis_size(axis), x.shape[dim])
        up = [(i, (i + 1) % devices) for i in range(devices - 1)]
        down = [(j, i) for i, j in up]
        last = lax.slice_in_dim(x, length - width, length, axis=dim)
        first = lax.slice_in_dim(x, 0, width, axis=dim)
        before = lax.ppermute(last, axis, up)
        after = lax.ppermute(first, axis, down)
        x = jnp.concatenate([before, x, after], axis=dim)
    return x


def input_conv(padded, kernel):
    out_rows = padded.shape[0] - 2
    col_count = padded.shape[2]
    wide = jnp.pad(padded, ((0, 0), (0, 0), (1, 1)))
    shifted = jnp.concatenate(
        [wide[i : i + out_rows, :, j : j + col_count] for i in range(3) for j in range(3)], axis=1
    )
    return jnp.einsum(
        "rkw,kc->rwc",
        shifted,
        kernel.reshape(-1, kernel.shape[3]),
        preferred_element_type=jnp.float32,
    )


def feature_conv(padded, kernel):
    out_rows = padded.shape[1] - 2
    col_count = padded.shape[2]
    wide = jnp.pad(padded, ((0, 0), (0, 0), (1, 1), (0, 0)))
    shifted = jnp.concatenate([wide[:, :, j : j + col_count] for j in range(3)], axis=3)
    summed = jnp.zeros((padded.shape[0], out_rows, col_count, kernel.shape[3]), jnp.float32)
    for i in range(3):
        summed = summed + jnp.einsum(
            "mrwc,cd->mrwd",
            shifted[:, i : i + out_rows],
            kernel[i].reshape(-1, kernel.shape[3]),
            preferred_element_type=jnp.float32,
        )
    return summed


def condition(base, cond_scale, cond_shift):
    average = jnp.mean(base, axis=-1, keepdims=True)
    centred = base - average
    spread = jnp.mean(centred * centred, axis=-1, keepdims=True)
    normed = centred * lax.rsqrt(spread + 1e-05)
    mixed = normed[None] * (1.0 + cond_scale[:, None, None, :]) + cond_shift[:, None, None, :]
    return jax.nn.gelu(mixed).astype(jnp.bfloat16)


def abs_terms(probe, sample_group_predictions):

    def abs_single(member_index):
        return jnp.sum(jnp.abs(member_index[None] - sample_group_predictions), axis=0)

    return lax.map(abs_single, probe)


def sign_terms(probe, sample_group_predictions):

    def sign_single(member_index):
        return jnp.sum(jnp.sign(member_index[None] - sample_group_predictions), axis=0)

    return lax.map(sign_single, probe)


def all_reduce_sum(parts):
    peers = ("group", "tile")
    devices = lax.axis_size("group") * lax.axis_size("tile")
    flat = jnp.concatenate([p.reshape(-1) for p in parts])
    total = flat.shape[0]
    width = -(-total // (2 * devices * 128)) * 128
    flat = jnp.pad(flat, (0, 2 * width * devices - total)).reshape(2, devices * width)
    core = lax.axis_index("core")
    swap = [(0, 1), (1, 0)]
    first = core == 0
    keep = jnp.where(first, flat[0], flat[1])
    half = keep + lax.ppermute(jnp.where(first, flat[1], flat[0]), "core", swap)
    pieces = lax.all_to_all(half.reshape(devices, width), peers, 0, 0, tiled=True)
    own = jnp.sum(pieces, axis=0, keepdims=True)
    summed = lax.all_to_all(jnp.broadcast_to(own, (devices, width)), peers, 0, 0, tiled=True)
    summed = summed.reshape(-1)
    other = lax.ppermute(summed, "core", swap)
    spread = jnp.where(first, jnp.concatenate([summed, other]), jnp.concatenate([other, summed]))
    out, at = [], 0
    for p in parts:
        out.append(spread[at : at + p.size].reshape(p.shape))
        at += p.size
    return tuple(out)


def on_device(
    upsampled_coarse,
    target,
    seeds,
    band_row,
    noise_bank,
    cond_weight,
    conv_in,
    conv_mid,
    conv_out,
    head_weight,
    per_quantity_offset,
):
    channels = conv_mid.shape[3]
    row_count = upsampled_coarse.shape[0]
    var_count = upsampled_coarse.shape[1]
    col_count = upsampled_coarse.shape[2]
    tile_count = lax.axis_size("tile")
    tile_at = lax.axis_index("tile")
    band_rows = row_count * tile_count
    selector = (seeds[:, None] == jnp.arange(noise_bank.shape[0], dtype=jnp.int32)[None]).astype(
        jnp.float32
    )
    noise_vec = jnp.dot(selector, noise_bank, precision=lax.Precision.HIGHEST)
    random_latent_gain = jnp.dot(noise_vec, cond_weight, precision=lax.Precision.HIGHEST)
    cond_scale = random_latent_gain[:, :channels]
    cond_shift = random_latent_gain[:, channels:]
    input_padded = extended(upsampled_coarse, (("tile", 0),), 3)
    band_at = tile_at * row_count + jnp.arange(-2, row_count + 2, dtype=jnp.int32)
    inside = ((band_at >= 0) & (band_at < band_rows))[None, :, None, None]
    first_wide = condition(input_conv(input_padded, conv_in), cond_scale, cond_shift)
    first_wide = jnp.where(inside, first_wide, jnp.zeros_like(first_wide))
    first_hidden = first_wide[:, 2 : 2 + row_count]
    second_padded = jax.nn.gelu(feature_conv(first_wide, conv_mid)).astype(jnp.bfloat16)
    second_padded = jnp.where(inside[:, 1:-1], second_padded, jnp.zeros_like(second_padded))
    final_linear_response = feature_conv(second_padded, conv_out)
    latent_layer_three = (
        first_hidden.astype(jnp.float32) + jax.nn.gelu(final_linear_response)
    ).astype(jnp.bfloat16)
    final_layer_result = jnp.einsum(
        "mrwc,cv->vmrw", latent_layer_three, head_weight, preferred_element_type=jnp.float32
    )
    sample_prediction = (
        final_layer_result
        + jnp.transpose(upsampled_coarse, (1, 0, 2)).astype(jnp.float32)[:, None]
        + per_quantity_offset[:, None, None, None]
    ).astype(jnp.bfloat16)
    row_global = band_row[0] + tile_at * row_count + jnp.arange(row_count, dtype=jnp.int32)
    latitude = math.pi * (row_global.astype(jnp.float32) + 0.5) / GRID_ROWS - math.pi / 2
    row_factor = (jnp.cos(latitude) / (band_rows * col_count))[None, None, :, None]
    var_share = var_count // (lax.axis_size("group") * lax.axis_size("core"))
    var_start = lax.axis_index(MEMBER) * var_share
    collected_members = lax.all_to_all(
        sample_prediction, MEMBER, split_axis=0, concat_axis=1, tiled=True
    )
    sample_group_predictions = collected_members.astype(jnp.float32)
    member_count = sample_group_predictions.shape[1]
    truth = jnp.transpose(
        lax.dynamic_slice_in_dim(target, var_start, var_share, 1), (1, 0, 2)
    ).astype(jnp.float32)[:, None]
    pair_differ = sample_group_predictions[:, :, None] - sample_group_predictions[:, None, :]
    abs_sums = jnp.sum(jnp.abs(pair_differ), axis=2)
    sign_sums = jnp.sum(jnp.sign(pair_differ), axis=2)
    crps_share = jnp.mean(jnp.abs(sample_group_predictions - truth), axis=1) - jnp.sum(
        abs_sums, axis=1
    ) / (2 * member_count * (member_count - 1))
    crps_map = jnp.transpose(crps_share, (1, 0, 2))
    cot_share = (
        row_factor
        * (
            jnp.sign(sample_group_predictions - truth) / member_count
            - sign_sums / (member_count * (member_count - 1))
        )
    ).astype(jnp.bfloat16)
    cotangent = lax.all_to_all(cot_share, MEMBER, split_axis=1, concat_axis=0, tiled=True)
    head_grad = jnp.einsum(
        "mrwc,vmrw->cv", latent_layer_three, cotangent, preferred_element_type=jnp.float32
    )
    bias_grad = jnp.sum(cotangent.astype(jnp.float32), axis=(1, 2, 3))
    back = jnp.einsum("vmrw,cv->mrwc", cotangent, head_weight, preferred_element_type=jnp.float32)
    unused_out, pullback = jax.vjp(jax.nn.gelu, final_linear_response)
    d_pre = pullback(back)[0].astype(jnp.bfloat16)
    second_wide = jnp.pad(second_padded, ((0, 0), (0, 0), (1, 1), (0, 0)))
    rows_of = []
    for i in range(3):
        cols_of = []
        for j in range(3):
            cols_of.append(
                jnp.einsum(
                    "mrwc,mrwd->cd",
                    second_wide[:, i : i + row_count, j : j + col_count],
                    d_pre,
                    preferred_element_type=jnp.float32,
                )
            )
        rows_of.append(jnp.stack(cols_of))
    conv_grad = jnp.stack(rows_of)
    conv_grad, head_grad_t, bias_grad = all_reduce_sum((conv_grad, head_grad.T, bias_grad))
    head_grad = head_grad_t.T
    return (crps_map, conv_grad, head_grad, bias_grad)


def solution(mesh):
    members = mesh.shape["member"]
    split = Mesh(
        mesh.devices.reshape(members // 2, 2, mesh.shape["tile"]), ("group", "core", "tile")
    )
    return jax.shard_map(
        on_device,
        mesh=split,
        in_specs=(
            P("tile", None, None),
            P("tile", None, None),
            P(MEMBER),
            P(),
            P(),
            P(),
            P(),
            P(),
            P(),
            P(),
            P(),
        ),
        out_specs=(P("tile", MEMBER, None), P(), P(), P()),
        check_vma=False,
    )
```

```python
import math

import jax
import jax.numpy as jnp
from jax import lax
from jax.sharding import Mesh, PartitionSpec as P

GRID_ROWS = 2048
MEMBER = ("group", "core")


def extended(x, sides, width):
    for axis, dim in sides:
        devices, length = (lax.axis_size(axis), x.shape[dim])
        up = [(i, (i + 1) % devices) for i in range(devices - 1)]
        down = [(j, i) for i, j in up]
        last = lax.slice_in_dim(x, length - width, length, axis=dim)
        first = lax.slice_in_dim(x, 0, width, axis=dim)
        before = lax.ppermute(last, axis, up)
        after = lax.ppermute(first, axis, down)
        x = jnp.concatenate([before, x, after], axis=dim)
    return x


def input_conv(padded, kernel):
    out_rows = padded.shape[0] - 2
    col_count = padded.shape[2]
    wide = jnp.pad(padded, ((0, 0), (0, 0), (1, 1)))
    shifted = jnp.concatenate(
        [wide[i : i + out_rows, :, j : j + col_count] for i in range(3) for j in range(3)], axis=1
    )
    return jnp.einsum(
        "rkw,kc->rwc",
        shifted,
        kernel.reshape(-1, kernel.shape[3]),
        preferred_element_type=jnp.float32,
    )


def feature_conv(padded, kernel):
    out_rows = padded.shape[1] - 2
    col_count = padded.shape[2]
    wide = jnp.pad(padded, ((0, 0), (0, 0), (1, 1), (0, 0)))
    shifted = jnp.concatenate([wide[:, :, j : j + col_count] for j in range(3)], axis=3)
    summed = jnp.zeros((padded.shape[0], out_rows, col_count, kernel.shape[3]), jnp.float32)
    for i in range(3):
        summed = summed + jnp.einsum(
            "mrwc,cd->mrwd",
            shifted[:, i : i + out_rows],
            kernel[i].reshape(-1, kernel.shape[3]),
            preferred_element_type=jnp.float32,
        )
    return summed


def condition(base, cond_scale, cond_shift):
    average = jnp.mean(base, axis=-1, keepdims=True)
    centred = base - average
    spread = jnp.mean(centred * centred, axis=-1, keepdims=True)
    normed = centred * lax.rsqrt(spread + 1e-05)
    mixed = normed[None] * (1.0 + cond_scale[:, None, None, :]) + cond_shift[:, None, None, :]
    return jax.nn.gelu(mixed).astype(jnp.bfloat16)


def abs_terms(probe, sample_group_predictions):

    def abs_single(member_index):
        return jnp.sum(jnp.abs(member_index[None] - sample_group_predictions), axis=0)

    return lax.map(abs_single, probe)


def sign_terms(probe, sample_group_predictions):

    def sign_single(member_index):
        return jnp.sum(jnp.sign(member_index[None] - sample_group_predictions), axis=0)

    return lax.map(sign_single, probe)


def all_reduce_sum(parts):
    peers = ("group", "tile")
    devices = lax.axis_size("group") * lax.axis_size("tile")
    flat = jnp.concatenate([p.reshape(-1) for p in parts])
    total = flat.shape[0]
    width = -(-total // (2 * devices * 128)) * 128
    flat = jnp.pad(flat, (0, 2 * width * devices - total)).reshape(2, devices * width)
    core = lax.axis_index("core")
    swap = [(0, 1), (1, 0)]
    first = core == 0
    keep = jnp.where(first, flat[0], flat[1])
    half = keep + lax.ppermute(jnp.where(first, flat[1], flat[0]), "core", swap)
    pieces = lax.all_to_all(half.reshape(devices, width), peers, 0, 0, tiled=True)
    own = jnp.sum(pieces, axis=0, keepdims=True)
    summed = lax.all_to_all(jnp.broadcast_to(own, (devices, width)), peers, 0, 0, tiled=True)
    summed = summed.reshape(-1)
    other = lax.ppermute(summed, "core", swap)
    spread = jnp.where(first, jnp.concatenate([summed, other]), jnp.concatenate([other, summed]))
    out, at = [], 0
    for p in parts:
        out.append(spread[at : at + p.size].reshape(p.shape))
        at += p.size
    return tuple(out)


def on_device(
    upsampled_coarse,
    target,
    seeds,
    band_row,
    noise_bank,
    cond_weight,
    conv_in,
    conv_mid,
    conv_out,
    head_weight,
    per_quantity_offset,
):
    channels = conv_mid.shape[3]
    row_count = upsampled_coarse.shape[0]
    var_count = upsampled_coarse.shape[1]
    col_count = upsampled_coarse.shape[2]
    tile_count = lax.axis_size("tile")
    tile_at = lax.axis_index("tile")
    band_rows = row_count * tile_count
    selector = (seeds[:, None] == jnp.arange(noise_bank.shape[0], dtype=jnp.int32)[None]).astype(
        jnp.float32
    )
    noise_vec = jnp.dot(selector, noise_bank, precision=lax.Precision.HIGHEST)
    random_latent_gain = jnp.dot(noise_vec, cond_weight, precision=lax.Precision.HIGHEST)
    cond_scale = random_latent_gain[:, :channels]
    cond_shift = random_latent_gain[:, channels:]
    input_padded = extended(upsampled_coarse, (("tile", 0),), 3)
    band_at = tile_at * row_count + jnp.arange(-2, row_count + 2, dtype=jnp.int32)
    inside = ((band_at >= 0) & (band_at < band_rows))[None, :, None, None]
    first_wide = condition(input_conv(input_padded, conv_in), cond_scale, cond_shift)
    first_wide = jnp.where(inside, first_wide, jnp.zeros_like(first_wide))
    first_hidden = first_wide[:, 2 : 2 + row_count]
    second_padded = jax.nn.gelu(feature_conv(first_wide, conv_mid)).astype(jnp.bfloat16)
    second_padded = jnp.where(inside[:, 1:-1], second_padded, jnp.zeros_like(second_padded))
    final_linear_response = feature_conv(second_padded, conv_out)
    latent_layer_three = (
        first_hidden.astype(jnp.float32) + jax.nn.gelu(final_linear_response)
    ).astype(jnp.bfloat16)
    final_layer_result = jnp.einsum(
        "mrwc,cv->vmrw", latent_layer_three, head_weight, preferred_element_type=jnp.float32
    )
    sample_prediction = (
        final_layer_result
        + jnp.transpose(upsampled_coarse, (1, 0, 2)).astype(jnp.float32)[:, None]
        + per_quantity_offset[:, None, None, None]
    ).astype(jnp.bfloat16)
    row_global = band_row[0] + tile_at * row_count + jnp.arange(row_count, dtype=jnp.int32)
    latitude = math.pi * (row_global.astype(jnp.float32) + 0.5) / GRID_ROWS - math.pi / 2
    row_factor = (jnp.cos(latitude) / (band_rows * col_count))[None, None, :, None]
    var_share = var_count // (lax.axis_size("group") * lax.axis_size("core"))
    var_start = lax.axis_index(MEMBER) * var_share
    collected_members = lax.all_to_all(
        sample_prediction, MEMBER, split_axis=0, concat_axis=1, tiled=True
    )
    sample_group_predictions = collected_members.astype(jnp.float32)
    member_count = sample_group_predictions.shape[1]
    truth = jnp.transpose(
        lax.dynamic_slice_in_dim(target, var_start, var_share, 1), (1, 0, 2)
    ).astype(jnp.float32)[:, None]
    pair_differ = sample_group_predictions[:, :, None] - sample_group_predictions[:, None, :]
    sign_sums = jnp.sum(jnp.sign(pair_differ), axis=2)
    scored, scored_truth = lax.optimization_barrier((sample_group_predictions, truth))
    abs_sums = jnp.sum(jnp.abs(scored[:, :, None] - scored[:, None, :]), axis=2)
    crps_share = jnp.mean(jnp.abs(scored - scored_truth), axis=1) - jnp.sum(
        abs_sums, axis=1
    ) / (2 * member_count * (member_count - 1))
    crps_map = jnp.transpose(crps_share, (1, 0, 2))
    cot_share = (
        row_factor
        * (
            jnp.sign(sample_group_predictions - truth) / member_count
            - sign_sums / (member_count * (member_count - 1))
        )
    ).astype(jnp.bfloat16)
    cotangent = lax.all_to_all(cot_share, MEMBER, split_axis=1, concat_axis=0, tiled=True)
    head_grad = jnp.einsum(
        "mrwc,vmrw->cv", latent_layer_three, cotangent, preferred_element_type=jnp.float32
    )
    bias_grad = jnp.sum(cotangent.astype(jnp.float32), axis=(1, 2, 3))
    back = jnp.einsum("vmrw,cv->mrwc", cotangent, head_weight, preferred_element_type=jnp.float32)
    unused_out, pullback = jax.vjp(jax.nn.gelu, final_linear_response)
    d_pre = pullback(back)[0].astype(jnp.bfloat16)
    second_wide = jnp.pad(second_padded, ((0, 0), (0, 0), (1, 1), (0, 0)))
    rows_of = []
    for i in range(3):
        cols_of = []
        for j in range(3):
            cols_of.append(
                jnp.einsum(
                    "mrwc,mrwd->cd",
                    second_wide[:, i : i + row_count, j : j + col_count],
                    d_pre,
                    preferred_element_type=jnp.float32,
                )
            )
        rows_of.append(jnp.stack(cols_of))
    conv_grad = jnp.stack(rows_of)
    conv_grad, head_grad_t, bias_grad = all_reduce_sum((conv_grad, head_grad.T, bias_grad))
    head_grad = head_grad_t.T
    return (crps_map, conv_grad, head_grad, bias_grad)


def solution(mesh):
    members = mesh.shape["member"]
    split = Mesh(
        mesh.devices.reshape(members // 2, 2, mesh.shape["tile"]), ("group", "core", "tile")
    )
    return jax.shard_map(
        on_device,
        mesh=split,
        in_specs=(
            P("tile", None, None),
            P("tile", None, None),
            P(MEMBER),
            P(),
            P(),
            P(),
            P(),
            P(),
            P(),
            P(),
            P(),
        ),
        out_specs=(P("tile", MEMBER, None), P(), P(), P()),
        check_vma=False,
    )
```

```python
import math

import jax
import jax.numpy as jnp
from jax import lax
from jax.sharding import Mesh, PartitionSpec as P

GRID_ROWS = 2048
MEMBER = ("group", "core")


def extended(x, sides, width):
    for axis, dim in sides:
        devices, length = (lax.axis_size(axis), x.shape[dim])
        up = [(i, (i + 1) % devices) for i in range(devices - 1)]
        down = [(j, i) for i, j in up]
        before = lax.slice_in_dim(lax.ppermute(x, axis, up), length - width, length, axis=dim)
        after = lax.slice_in_dim(lax.ppermute(x, axis, down), 0, width, axis=dim)
        x = jnp.concatenate([before, x, after], axis=dim)
    return x


def input_conv(padded, kernel):
    out_rows = padded.shape[0] - 2
    col_count = padded.shape[2]
    wide = jnp.pad(padded, ((0, 0), (0, 0), (1, 1)))
    shifted = jnp.concatenate(
        [wide[i : i + out_rows, :, j : j + col_count] for i in range(3) for j in range(3)], axis=1
    )
    return jnp.einsum(
        "rkw,kc->rwc",
        shifted,
        kernel.reshape(-1, kernel.shape[3]),
        preferred_element_type=jnp.float32,
    )


def feature_conv(padded, kernel):
    out_rows = padded.shape[1] - 2
    col_count = padded.shape[2]
    wide = jnp.pad(padded, ((0, 0), (0, 0), (1, 1), (0, 0)))
    shifted = jnp.concatenate([wide[:, :, j : j + col_count] for j in range(3)], axis=3)
    summed = jnp.zeros((padded.shape[0], out_rows, col_count, kernel.shape[3]), jnp.float32)
    for i in range(3):
        summed = summed + jnp.einsum(
            "mrwc,cd->mrwd",
            shifted[:, i : i + out_rows],
            kernel[i].reshape(-1, kernel.shape[3]),
            preferred_element_type=jnp.float32,
        )
    return summed


def condition(base, cond_scale, cond_shift):
    average = jnp.mean(base, axis=-1, keepdims=True)
    centred = base - average
    spread = jnp.mean(centred * centred, axis=-1, keepdims=True)
    normed = centred * lax.rsqrt(spread + 1e-05)
    mixed = normed[None] * (1.0 + cond_scale[:, None, None, :]) + cond_shift[:, None, None, :]
    return jax.nn.gelu(mixed).astype(jnp.bfloat16)


def abs_terms(probe, sample_group_predictions):

    def abs_single(member_index):
        return jnp.sum(jnp.abs(member_index[None] - sample_group_predictions), axis=0)

    return lax.map(abs_single, probe)


def sign_terms(probe, sample_group_predictions):

    def sign_single(member_index):
        return jnp.sum(jnp.sign(member_index[None] - sample_group_predictions), axis=0)

    return lax.map(sign_single, probe)


def all_reduce_sum(parts):
    peers = ("group", "tile")
    devices = lax.axis_size("group") * lax.axis_size("tile")
    flat = jnp.concatenate([p.reshape(-1) for p in parts])
    total = flat.shape[0]
    width = -(-total // (2 * devices * 128)) * 128
    flat = jnp.pad(flat, (0, 2 * width * devices - total)).reshape(2, devices * width)
    core = lax.axis_index("core")
    swap = [(0, 1), (1, 0)]
    first = core == 0
    keep = jnp.where(first, flat[0], flat[1])
    half = keep + lax.ppermute(jnp.where(first, flat[1], flat[0]), "core", swap)
    pieces = lax.all_to_all(half.reshape(devices, width), peers, 0, 0, tiled=True)
    own = jnp.sum(pieces, axis=0, keepdims=True)
    summed = lax.all_to_all(jnp.broadcast_to(own, (devices, width)), peers, 0, 0, tiled=True)
    summed = summed.reshape(-1)
    other = lax.ppermute(summed, "core", swap)
    spread = jnp.where(first, jnp.concatenate([summed, other]), jnp.concatenate([other, summed]))
    out, at = [], 0
    for p in parts:
        out.append(spread[at : at + p.size].reshape(p.shape))
        at += p.size
    return tuple(out)


def on_device(
    upsampled_coarse,
    target,
    seeds,
    band_row,
    noise_bank,
    cond_weight,
    conv_in,
    conv_mid,
    conv_out,
    head_weight,
    per_quantity_offset,
):
    channels = conv_mid.shape[3]
    row_count = upsampled_coarse.shape[0]
    var_count = upsampled_coarse.shape[1]
    col_count = upsampled_coarse.shape[2]
    tile_count = lax.axis_size("tile")
    tile_at = lax.axis_index("tile")
    band_rows = row_count * tile_count
    selector = (seeds[:, None] == jnp.arange(noise_bank.shape[0], dtype=jnp.int32)[None]).astype(
        jnp.float32
    )
    noise_vec = jnp.dot(selector, noise_bank, precision=lax.Precision.HIGHEST)
    random_latent_gain = jnp.dot(noise_vec, cond_weight, precision=lax.Precision.HIGHEST)
    cond_scale = random_latent_gain[:, :channels]
    cond_shift = random_latent_gain[:, channels:]
    input_padded = extended(upsampled_coarse, (("tile", 0),), 3)
    band_at = tile_at * row_count + jnp.arange(-2, row_count + 2, dtype=jnp.int32)
    inside = ((band_at >= 0) & (band_at < band_rows))[None, :, None, None]
    first_wide = condition(input_conv(input_padded, conv_in), cond_scale, cond_shift)
    first_wide = jnp.where(inside, first_wide, jnp.zeros_like(first_wide))
    first_hidden = first_wide[:, 2 : 2 + row_count]
    second_padded = jax.nn.gelu(feature_conv(first_wide, conv_mid)).astype(jnp.bfloat16)
    second_padded = jnp.where(inside[:, 1:-1], second_padded, jnp.zeros_like(second_padded))
    final_linear_response = feature_conv(second_padded, conv_out)
    latent_layer_three = (
        first_hidden.astype(jnp.float32) + jax.nn.gelu(final_linear_response)
    ).astype(jnp.bfloat16)
    final_layer_result = jnp.einsum(
        "mrwc,cv->vmrw", latent_layer_three, head_weight, preferred_element_type=jnp.float32
    )
    sample_prediction = (
        final_layer_result
        + jnp.transpose(upsampled_coarse, (1, 0, 2)).astype(jnp.float32)[:, None]
        + per_quantity_offset[:, None, None, None]
    ).astype(jnp.bfloat16)
    row_global = band_row[0] + tile_at * row_count + jnp.arange(row_count, dtype=jnp.int32)
    latitude = math.pi * (row_global.astype(jnp.float32) + 0.5) / GRID_ROWS - math.pi / 2
    row_factor = (jnp.cos(latitude) / (band_rows * col_count))[None, None, :, None]
    var_share = var_count // (lax.axis_size("group") * lax.axis_size("core"))
    var_start = lax.axis_index(MEMBER) * var_share
    collected_members = lax.all_to_all(
        sample_prediction, MEMBER, split_axis=0, concat_axis=1, tiled=True
    )
    sample_group_predictions = collected_members.astype(jnp.float32)
    member_count = sample_group_predictions.shape[1]
    truth = jnp.transpose(
        lax.dynamic_slice_in_dim(target, var_start, var_share, 1), (1, 0, 2)
    ).astype(jnp.float32)[:, None]
    pair_differ = sample_group_predictions[:, :, None] - sample_group_predictions[:, None, :]
    abs_sums = jnp.sum(jnp.abs(pair_differ), axis=2)
    sign_sums = jnp.sum(jnp.sign(pair_differ), axis=2)
    crps_share = jnp.mean(jnp.abs(sample_group_predictions - truth), axis=1) - jnp.sum(
        abs_sums, axis=1
    ) / (2 * member_count * (member_count - 1))
    crps_map = jnp.transpose(crps_share, (1, 0, 2))
    cot_share = (
        row_factor
        * (
            jnp.sign(sample_group_predictions - truth) / member_count
            - sign_sums / (member_count * (member_count - 1))
        )
    ).astype(jnp.bfloat16)
    cotangent = lax.all_to_all(cot_share, MEMBER, split_axis=1, concat_axis=0, tiled=True)
    head_grad = jnp.einsum(
        "mrwc,vmrw->cv", latent_layer_three, cotangent, preferred_element_type=jnp.float32
    )
    bias_grad = jnp.sum(cotangent.astype(jnp.float32), axis=(1, 2, 3))
    back = jnp.einsum("vmrw,cv->mrwc", cotangent, head_weight, preferred_element_type=jnp.float32)
    unused_out, pullback = jax.vjp(jax.nn.gelu, final_linear_response)
    d_pre = pullback(back)[0].astype(jnp.bfloat16)
    second_wide = jnp.pad(second_padded, ((0, 0), (0, 0), (1, 1), (0, 0)))
    rows_of = []
    for i in range(3):
        cols_of = []
        for j in range(3):
            cols_of.append(
                jnp.einsum(
                    "mrwc,mrwd->cd",
                    second_wide[:, i : i + row_count, j : j + col_count],
                    d_pre,
                    preferred_element_type=jnp.float32,
                )
            )
        rows_of.append(jnp.stack(cols_of))
    conv_grad = jnp.stack(rows_of)
    conv_grad, head_grad_t, bias_grad = all_reduce_sum((conv_grad, head_grad.T, bias_grad))
    head_grad = head_grad_t.T
    return (crps_map, conv_grad, head_grad, bias_grad)


def solution(mesh):
    members = mesh.shape["member"]
    split = Mesh(
        mesh.devices.reshape(members // 2, 2, mesh.shape["tile"]), ("group", "core", "tile")
    )
    return jax.shard_map(
        on_device,
        mesh=split,
        in_specs=(
            P("tile", None, None),
            P("tile", None, None),
            P(MEMBER),
            P(),
            P(),
            P(),
            P(),
            P(),
            P(),
            P(),
            P(),
        ),
        out_specs=(P("tile", MEMBER, None), P(), P(), P()),
        check_vma=False,
    )
```

```python
import math

import jax
import jax.numpy as jnp
from jax import lax
from jax.sharding import Mesh, PartitionSpec as P

GRID_ROWS = 2048
MEMBER = ("group", "core")


def extended(x, sides, width):
    for axis, dim in sides:
        devices, length = (lax.axis_size(axis), x.shape[dim])
        up = [(i, (i + 1) % devices) for i in range(devices - 1)]
        down = [(j, i) for i, j in up]
        before = lax.slice_in_dim(lax.ppermute(x, axis, up), length - width, length, axis=dim)
        after = lax.slice_in_dim(lax.ppermute(x, axis, down), 0, width, axis=dim)
        x = jnp.concatenate([before, x, after], axis=dim)
    return x


def input_conv(padded, kernel):
    out_rows = padded.shape[0] - 2
    col_count = padded.shape[2]
    wide = jnp.pad(padded, ((0, 0), (0, 0), (1, 1)))
    shifted = jnp.concatenate(
        [wide[i : i + out_rows, :, j : j + col_count] for i in range(3) for j in range(3)], axis=1
    )
    return jnp.einsum(
        "rkw,kc->rwc",
        shifted,
        kernel.reshape(-1, kernel.shape[3]),
        preferred_element_type=jnp.float32,
    )


def feature_conv(padded, kernel):
    out_rows = padded.shape[1] - 2
    col_count = padded.shape[2]
    wide = jnp.pad(padded, ((0, 0), (0, 0), (1, 1), (0, 0)))
    shifted = jnp.concatenate([wide[:, :, j : j + col_count] for j in range(3)], axis=3)
    summed = jnp.zeros((padded.shape[0], out_rows, col_count, kernel.shape[3]), jnp.float32)
    for i in range(3):
        summed = summed + jnp.einsum(
            "mrwc,cd->mrwd",
            shifted[:, i : i + out_rows],
            kernel[i].reshape(-1, kernel.shape[3]),
            preferred_element_type=jnp.float32,
        )
    return summed


def condition(base, cond_scale, cond_shift):
    average = jnp.mean(base, axis=-1, keepdims=True)
    centred = base - average
    spread = jnp.mean(centred * centred, axis=-1, keepdims=True)
    normed = centred * lax.rsqrt(spread + 1e-05)
    mixed = normed[None] * (1.0 + cond_scale[:, None, None, :]) + cond_shift[:, None, None, :]
    return jax.nn.gelu(mixed).astype(jnp.bfloat16)


def abs_terms(probe, sample_group_predictions):

    def abs_single(member_index):
        return jnp.sum(jnp.abs(member_index[None] - sample_group_predictions), axis=0)

    return lax.map(abs_single, probe)


def sign_terms(probe, sample_group_predictions):

    def sign_single(member_index):
        return jnp.sum(jnp.sign(member_index[None] - sample_group_predictions), axis=0)

    return lax.map(sign_single, probe)


def all_reduce_sum(parts):
    peers = ("group", "tile")
    devices = lax.axis_size("group") * lax.axis_size("tile")
    flat = jnp.concatenate([p.reshape(-1) for p in parts])
    total = flat.shape[0]
    width = -(-total // (2 * devices * 128)) * 128
    flat = jnp.pad(flat, (0, 2 * width * devices - total)).reshape(2, devices * width)
    core = lax.axis_index("core")
    swap = [(0, 1), (1, 0)]
    first = core == 0
    keep = jnp.where(first, flat[0], flat[1])
    half = keep + lax.ppermute(jnp.where(first, flat[1], flat[0]), "core", swap)
    pieces = lax.all_to_all(half.reshape(devices, width), peers, 0, 0, tiled=True)
    own = jnp.sum(pieces, axis=0, keepdims=True)
    summed = lax.all_to_all(jnp.broadcast_to(own, (devices, width)), peers, 0, 0, tiled=True)
    summed = summed.reshape(-1)
    other = lax.ppermute(summed, "core", swap)
    spread = jnp.where(first, jnp.concatenate([summed, other]), jnp.concatenate([other, summed]))
    out, at = [], 0
    for p in parts:
        out.append(spread[at : at + p.size].reshape(p.shape))
        at += p.size
    return tuple(out)


def on_device(
    upsampled_coarse,
    target,
    seeds,
    band_row,
    noise_bank,
    cond_weight,
    conv_in,
    conv_mid,
    conv_out,
    head_weight,
    per_quantity_offset,
):
    channels = conv_mid.shape[3]
    row_count = upsampled_coarse.shape[0]
    var_count = upsampled_coarse.shape[1]
    col_count = upsampled_coarse.shape[2]
    tile_count = lax.axis_size("tile")
    tile_at = lax.axis_index("tile")
    band_rows = row_count * tile_count
    selector = (seeds[:, None] == jnp.arange(noise_bank.shape[0], dtype=jnp.int32)[None]).astype(
        jnp.float32
    )
    noise_vec = jnp.dot(selector, noise_bank, precision=lax.Precision.HIGHEST)
    random_latent_gain = jnp.dot(noise_vec, cond_weight, precision=lax.Precision.HIGHEST)
    cond_scale = random_latent_gain[:, :channels]
    cond_shift = random_latent_gain[:, channels:]
    input_padded = extended(upsampled_coarse, (("tile", 0),), 3)
    band_at = tile_at * row_count + jnp.arange(-2, row_count + 2, dtype=jnp.int32)
    inside = ((band_at >= 0) & (band_at < band_rows))[None, :, None, None]
    first_wide = condition(input_conv(input_padded, conv_in), cond_scale, cond_shift)
    first_wide = jnp.where(inside, first_wide, jnp.zeros_like(first_wide))
    first_hidden = first_wide[:, 2 : 2 + row_count]
    second_padded = jax.nn.gelu(feature_conv(first_wide, conv_mid)).astype(jnp.bfloat16)
    second_padded = jnp.where(inside[:, 1:-1], second_padded, jnp.zeros_like(second_padded))
    final_linear_response = feature_conv(second_padded, conv_out)
    latent_layer_three = (
        first_hidden.astype(jnp.float32) + jax.nn.gelu(final_linear_response)
    ).astype(jnp.bfloat16)
    final_layer_result = jnp.einsum(
        "mrwc,cv->vmrw", latent_layer_three, head_weight, preferred_element_type=jnp.float32
    )
    sample_prediction = (
        final_layer_result
        + jnp.transpose(upsampled_coarse, (1, 0, 2)).astype(jnp.float32)[:, None]
        + per_quantity_offset[:, None, None, None]
    ).astype(jnp.bfloat16)
    row_global = band_row[0] + tile_at * row_count + jnp.arange(row_count, dtype=jnp.int32)
    latitude = math.pi * (row_global.astype(jnp.float32) + 0.5) / GRID_ROWS - math.pi / 2
    row_factor = (jnp.cos(latitude) / (band_rows * col_count))[None, None, :, None]
    var_share = var_count // (lax.axis_size("group") * lax.axis_size("core"))
    var_start = lax.axis_index(MEMBER) * var_share
    collected_members = lax.all_to_all(
        sample_prediction, MEMBER, split_axis=0, concat_axis=1, tiled=True
    )
    sample_group_predictions = collected_members.astype(jnp.float32)
    member_count = sample_group_predictions.shape[1]
    truth = jnp.transpose(
        lax.dynamic_slice_in_dim(target, var_start, var_share, 1), (1, 0, 2)
    ).astype(jnp.float32)[:, None]
    pair_differ = sample_group_predictions[:, :, None] - sample_group_predictions[:, None, :]
    abs_sums = jnp.sum(jnp.abs(pair_differ), axis=2)
    sign_sums = jnp.sum(jnp.sign(pair_differ), axis=2)
    crps_share = jnp.mean(jnp.abs(sample_group_predictions - truth), axis=1) - jnp.sum(
        abs_sums, axis=1
    ) / (2 * member_count * (member_count - 1))
    crps_map = jnp.transpose(crps_share, (1, 0, 2))
    cot_share = (
        row_factor
        * (
            jnp.sign(sample_group_predictions - truth) / member_count
            - sign_sums / (member_count * (member_count - 1))
        )
    ).astype(jnp.bfloat16)
    cotangent = lax.all_to_all(cot_share, MEMBER, split_axis=1, concat_axis=0, tiled=True)
    head_grad = jnp.einsum(
        "mrwc,vmrw->cv", latent_layer_three, cotangent, preferred_element_type=jnp.float32
    )
    bias_grad = jnp.sum(cotangent.astype(jnp.float32), axis=(1, 2, 3))
    back = jnp.einsum("vmrw,cv->mrwc", cotangent, head_weight, preferred_element_type=jnp.float32)
    unused_out, pullback = jax.vjp(jax.nn.gelu, final_linear_response)
    slope = lax.optimization_barrier(pullback(jnp.ones_like(final_linear_response))[0])
    d_pre = (back * slope).astype(jnp.bfloat16)
    second_wide = jnp.pad(second_padded, ((0, 0), (0, 0), (1, 1), (0, 0)))
    rows_of = []
    for i in range(3):
        cols_of = []
        for j in range(3):
            cols_of.append(
                jnp.einsum(
                    "mrwc,mrwd->cd",
                    second_wide[:, i : i + row_count, j : j + col_count],
                    d_pre,
                    preferred_element_type=jnp.float32,
                )
            )
        rows_of.append(jnp.stack(cols_of))
    conv_grad = jnp.stack(rows_of)
    conv_grad, head_grad_t, bias_grad = all_reduce_sum((conv_grad, head_grad.T, bias_grad))
    head_grad = head_grad_t.T
    return (crps_map, conv_grad, head_grad, bias_grad)


def solution(mesh):
    members = mesh.shape["member"]
    split = Mesh(
        mesh.devices.reshape(members // 2, 2, mesh.shape["tile"]), ("group", "core", "tile")
    )
    return jax.shard_map(
        on_device,
        mesh=split,
        in_specs=(
            P("tile", None, None),
            P("tile", None, None),
            P(MEMBER),
            P(),
            P(),
            P(),
            P(),
            P(),
            P(),
            P(),
            P(),
        ),
        out_specs=(P("tile", MEMBER, None), P(), P(), P()),
        check_vma=False,
    )
```

```python
import math

import jax
import jax.numpy as jnp
from jax import lax
from jax.sharding import Mesh, PartitionSpec as P

GRID_ROWS = 2048
MEMBER = ("group", "core")


def extended(x, sides, width):
    for axis, dim in sides:
        devices, length = (lax.axis_size(axis), x.shape[dim])
        up = [(i, (i + 1) % devices) for i in range(devices - 1)]
        down = [(j, i) for i, j in up]
        before = lax.slice_in_dim(lax.ppermute(x, axis, up), length - width, length, axis=dim)
        after = lax.slice_in_dim(lax.ppermute(x, axis, down), 0, width, axis=dim)
        x = jnp.concatenate([before, x, after], axis=dim)
    return x


def input_conv(padded, kernel):
    out_rows = padded.shape[0] - 2
    col_count = padded.shape[2]
    wide = jnp.pad(padded, ((0, 0), (0, 0), (1, 1)))
    shifted = jnp.concatenate(
        [wide[i : i + out_rows, :, j : j + col_count] for i in range(3) for j in range(3)], axis=1
    )
    return jnp.einsum(
        "rkw,kc->rwc",
        shifted,
        kernel.reshape(-1, kernel.shape[3]),
        preferred_element_type=jnp.float32,
    )


def feature_conv(padded, kernel):
    out_rows = padded.shape[1] - 2
    col_count = padded.shape[2]
    wide = jnp.pad(padded, ((0, 0), (0, 0), (1, 1), (0, 0)))
    shifted = jnp.concatenate([wide[:, :, j : j + col_count] for j in range(3)], axis=3)
    summed = jnp.zeros((padded.shape[0], out_rows, col_count, kernel.shape[3]), jnp.float32)
    for i in range(3):
        summed = summed + jnp.einsum(
            "mrwc,cd->mrwd",
            shifted[:, i : i + out_rows],
            kernel[i].reshape(-1, kernel.shape[3]),
            preferred_element_type=jnp.float32,
        )
    return summed


def condition(base, cond_scale, cond_shift):
    average = jnp.mean(base, axis=-1, keepdims=True)
    centred = base - average
    spread = jnp.mean(centred * centred, axis=-1, keepdims=True)
    normed = centred * lax.rsqrt(spread + 1e-05)
    mixed = normed[None] * (1.0 + cond_scale[:, None, None, :]) + cond_shift[:, None, None, :]
    return jax.nn.gelu(mixed).astype(jnp.bfloat16)


def abs_terms(probe, sample_group_predictions):

    def abs_single(member_index):
        return jnp.sum(jnp.abs(member_index[None] - sample_group_predictions), axis=0)

    return lax.map(abs_single, probe)


def sign_terms(probe, sample_group_predictions):

    def sign_single(member_index):
        return jnp.sum(jnp.sign(member_index[None] - sample_group_predictions), axis=0)

    return lax.map(sign_single, probe)


def all_reduce_sum(parts):
    peers = ("group", "tile")
    devices = lax.axis_size("group") * lax.axis_size("tile")
    flat = jnp.concatenate([p.reshape(-1) for p in parts])
    total = flat.shape[0]
    width = -(-total // (2 * devices * 128)) * 128
    flat = jnp.pad(flat, (0, 2 * width * devices - total)).reshape(2, devices * width)
    core = lax.axis_index("core")
    swap = [(0, 1), (1, 0)]
    first = core == 0
    keep = jnp.where(first, flat[0], flat[1])
    half = keep + lax.ppermute(jnp.where(first, flat[1], flat[0]), "core", swap)
    pieces = lax.all_to_all(half.reshape(devices, width), peers, 0, 0, tiled=True)
    own = jnp.sum(pieces, axis=0, keepdims=True)
    summed = lax.all_to_all(jnp.broadcast_to(own, (devices, width)), peers, 0, 0, tiled=True)
    summed = summed.reshape(-1)
    other = lax.ppermute(summed, "core", swap)
    spread = jnp.where(first, jnp.concatenate([summed, other]), jnp.concatenate([other, summed]))
    out, at = [], 0
    for p in parts:
        out.append(spread[at : at + p.size].reshape(p.shape))
        at += p.size
    return tuple(out)


def on_device(
    upsampled_coarse,
    target,
    seeds,
    band_row,
    noise_bank,
    cond_weight,
    conv_in,
    conv_mid,
    conv_out,
    head_weight,
    per_quantity_offset,
):
    channels = conv_mid.shape[3]
    row_count = upsampled_coarse.shape[0]
    var_count = upsampled_coarse.shape[1]
    col_count = upsampled_coarse.shape[2]
    tile_count = lax.axis_size("tile")
    tile_at = lax.axis_index("tile")
    band_rows = row_count * tile_count
    selector = (seeds[:, None] == jnp.arange(noise_bank.shape[0], dtype=jnp.int32)[None]).astype(
        jnp.float32
    )
    noise_vec = jnp.dot(selector, noise_bank, precision=lax.Precision.HIGHEST)
    random_latent_gain = jnp.dot(noise_vec, cond_weight, precision=lax.Precision.HIGHEST)
    cond_scale = random_latent_gain[:, :channels]
    cond_shift = random_latent_gain[:, channels:]
    input_padded = extended(upsampled_coarse, (("tile", 0),), 3)
    band_at = tile_at * row_count + jnp.arange(-2, row_count + 2, dtype=jnp.int32)
    inside = ((band_at >= 0) & (band_at < band_rows))[None, :, None, None]
    first_wide = condition(input_conv(input_padded, conv_in), cond_scale, cond_shift)
    first_wide = jnp.where(inside, first_wide, jnp.zeros_like(first_wide))
    first_hidden = first_wide[:, 2 : 2 + row_count]
    second_padded = jax.nn.gelu(feature_conv(first_wide, conv_mid)).astype(jnp.bfloat16)
    second_padded = jnp.where(inside[:, 1:-1], second_padded, jnp.zeros_like(second_padded))
    final_linear_response = feature_conv(second_padded, conv_out)
    latent_layer_three = (
        first_hidden.astype(jnp.float32) + jax.nn.gelu(final_linear_response)
    ).astype(jnp.bfloat16)
    final_layer_result = jnp.einsum(
        "mrwc,cv->vmrw", latent_layer_three, head_weight, preferred_element_type=jnp.float32
    )
    sample_prediction = (
        final_layer_result
        + jnp.transpose(upsampled_coarse, (1, 0, 2)).astype(jnp.float32)[:, None]
        + per_quantity_offset[:, None, None, None]
    ).astype(jnp.bfloat16)
    row_global = band_row[0] + tile_at * row_count + jnp.arange(row_count, dtype=jnp.int32)
    latitude = math.pi * (row_global.astype(jnp.float32) + 0.5) / GRID_ROWS - math.pi / 2
    row_factor = (jnp.cos(latitude) / (band_rows * col_count))[None, None, :, None]
    var_share = var_count // (lax.axis_size("group") * lax.axis_size("core"))
    var_start = lax.axis_index(MEMBER) * var_share
    collected_members = lax.all_to_all(
        sample_prediction, MEMBER, split_axis=0, concat_axis=1, tiled=True
    )
    sample_group_predictions = collected_members.astype(jnp.float32)
    member_count = sample_group_predictions.shape[1]
    truth = jnp.transpose(
        lax.dynamic_slice_in_dim(target, var_start, var_share, 1), (1, 0, 2)
    ).astype(jnp.float32)[:, None]
    pair_differ = sample_group_predictions[:, :, None] - sample_group_predictions[:, None, :]
    sign_sums = jnp.sum(jnp.sign(pair_differ), axis=2)
    scored, scored_truth = lax.optimization_barrier((sample_group_predictions, truth))
    abs_sums = jnp.sum(jnp.abs(scored[:, :, None] - scored[:, None, :]), axis=2)
    crps_share = jnp.mean(jnp.abs(scored - scored_truth), axis=1) - jnp.sum(
        abs_sums, axis=1
    ) / (2 * member_count * (member_count - 1))
    crps_map = jnp.transpose(crps_share, (1, 0, 2))
    cot_share = (
        row_factor
        * (
            jnp.sign(sample_group_predictions - truth) / member_count
            - sign_sums / (member_count * (member_count - 1))
        )
    ).astype(jnp.bfloat16)
    cotangent = lax.all_to_all(cot_share, MEMBER, split_axis=1, concat_axis=0, tiled=True)
    head_grad = jnp.einsum(
        "mrwc,vmrw->cv", latent_layer_three, cotangent, preferred_element_type=jnp.float32
    )
    bias_grad = jnp.sum(cotangent.astype(jnp.float32), axis=(1, 2, 3))
    back = jnp.einsum("vmrw,cv->mrwc", cotangent, head_weight, preferred_element_type=jnp.float32)
    unused_out, pullback = jax.vjp(jax.nn.gelu, final_linear_response)
    d_pre = pullback(back)[0].astype(jnp.bfloat16)
    second_wide = jnp.pad(second_padded, ((0, 0), (0, 0), (1, 1), (0, 0)))
    rows_of = []
    for i in range(3):
        cols_of = []
        for j in range(3):
            cols_of.append(
                jnp.einsum(
                    "mrwc,mrwd->cd",
                    second_wide[:, i : i + row_count, j : j + col_count],
                    d_pre,
                    preferred_element_type=jnp.float32,
                )
            )
        rows_of.append(jnp.stack(cols_of))
    conv_grad = jnp.stack(rows_of)
    conv_grad, head_grad_t, bias_grad = all_reduce_sum((conv_grad, head_grad.T, bias_grad))
    head_grad = head_grad_t.T
    return (crps_map, conv_grad, head_grad, bias_grad)


def solution(mesh):
    members = mesh.shape["member"]
    split = Mesh(
        mesh.devices.reshape(members // 2, 2, mesh.shape["tile"]), ("group", "core", "tile")
    )
    return jax.shard_map(
        on_device,
        mesh=split,
        in_specs=(
            P("tile", None, None),
            P("tile", None, None),
            P(MEMBER),
            P(),
            P(),
            P(),
            P(),
            P(),
            P(),
            P(),
            P(),
        ),
        out_specs=(P("tile", MEMBER, None), P(), P(), P()),
        check_vma=False,
    )
```

```python
import math

import jax
import jax.numpy as jnp
from jax import lax
from jax.sharding import Mesh, PartitionSpec as P

GRID_ROWS = 2048
MEMBER = ("group", "core")


def extended(x, sides, width):
    for axis, dim in sides:
        devices, length = (lax.axis_size(axis), x.shape[dim])
        up = [(i, (i + 1) % devices) for i in range(devices - 1)]
        down = [(j, i) for i, j in up]
        last = lax.slice_in_dim(x, length - width, length, axis=dim)
        first = lax.slice_in_dim(x, 0, width, axis=dim)
        before = lax.ppermute(last, axis, up)
        after = lax.ppermute(first, axis, down)
        x = jnp.concatenate([before, x, after], axis=dim)
    return x


def input_conv(padded, kernel):
    out_rows = padded.shape[0] - 2
    col_count = padded.shape[2]
    wide = jnp.pad(padded, ((0, 0), (0, 0), (1, 1)))
    shifted = jnp.concatenate(
        [wide[i : i + out_rows, :, j : j + col_count] for i in range(3) for j in range(3)], axis=1
    )
    return jnp.einsum(
        "rkw,kc->rwc",
        shifted,
        kernel.reshape(-1, kernel.shape[3]),
        preferred_element_type=jnp.float32,
    )


def feature_conv(padded, kernel):
    out_rows = padded.shape[1] - 2
    col_count = padded.shape[2]
    wide = jnp.pad(padded, ((0, 0), (0, 0), (1, 1), (0, 0)))
    shifted = jnp.concatenate([wide[:, :, j : j + col_count] for j in range(3)], axis=3)
    summed = jnp.zeros((padded.shape[0], out_rows, col_count, kernel.shape[3]), jnp.float32)
    for i in range(3):
        summed = summed + jnp.einsum(
            "mrwc,cd->mrwd",
            shifted[:, i : i + out_rows],
            kernel[i].reshape(-1, kernel.shape[3]),
            preferred_element_type=jnp.float32,
        )
    return summed


def condition(base, cond_scale, cond_shift):
    average = jnp.mean(base, axis=-1, keepdims=True)
    centred = base - average
    spread = jnp.mean(centred * centred, axis=-1, keepdims=True)
    normed = centred * lax.rsqrt(spread + 1e-05)
    mixed = normed[None] * (1.0 + cond_scale[:, None, None, :]) + cond_shift[:, None, None, :]
    return jax.nn.gelu(mixed).astype(jnp.bfloat16)


def abs_terms(probe, sample_group_predictions):

    def abs_single(member_index):
        return jnp.sum(jnp.abs(member_index[None] - sample_group_predictions), axis=0)

    return lax.map(abs_single, probe)


def sign_terms(probe, sample_group_predictions):

    def sign_single(member_index):
        return jnp.sum(jnp.sign(member_index[None] - sample_group_predictions), axis=0)

    return lax.map(sign_single, probe)


def all_reduce_sum(parts):
    peers = ("group", "tile")
    devices = lax.axis_size("group") * lax.axis_size("tile")
    flat = jnp.concatenate([p.reshape(-1) for p in parts])
    total = flat.shape[0]
    width = -(-total // (2 * devices * 128)) * 128
    flat = jnp.pad(flat, (0, 2 * width * devices - total)).reshape(2, devices * width)
    core = lax.axis_index("core")
    swap = [(0, 1), (1, 0)]
    first = core == 0
    keep = jnp.where(first, flat[0], flat[1])
    half = keep + lax.ppermute(jnp.where(first, flat[1], flat[0]), "core", swap)
    pieces = lax.all_to_all(half.reshape(devices, width), peers, 0, 0, tiled=True)
    own = jnp.sum(pieces, axis=0, keepdims=True)
    summed = lax.all_to_all(jnp.broadcast_to(own, (devices, width)), peers, 0, 0, tiled=True)
    summed = summed.reshape(-1)
    other = lax.ppermute(summed, "core", swap)
    spread = jnp.where(first, jnp.concatenate([summed, other]), jnp.concatenate([other, summed]))
    out, at = [], 0
    for p in parts:
        out.append(spread[at : at + p.size].reshape(p.shape))
        at += p.size
    return tuple(out)


def on_device(
    upsampled_coarse,
    target,
    seeds,
    band_row,
    noise_bank,
    cond_weight,
    conv_in,
    conv_mid,
    conv_out,
    head_weight,
    per_quantity_offset,
):
    channels = conv_mid.shape[3]
    row_count = upsampled_coarse.shape[0]
    var_count = upsampled_coarse.shape[1]
    col_count = upsampled_coarse.shape[2]
    tile_count = lax.axis_size("tile")
    tile_at = lax.axis_index("tile")
    band_rows = row_count * tile_count
    selector = (seeds[:, None] == jnp.arange(noise_bank.shape[0], dtype=jnp.int32)[None]).astype(
        jnp.float32
    )
    noise_vec = jnp.dot(selector, noise_bank, precision=lax.Precision.HIGHEST)
    random_latent_gain = jnp.dot(noise_vec, cond_weight, precision=lax.Precision.HIGHEST)
    cond_scale = random_latent_gain[:, :channels]
    cond_shift = random_latent_gain[:, channels:]
    input_padded = extended(upsampled_coarse, (("tile", 0),), 3)
    band_at = tile_at * row_count + jnp.arange(-2, row_count + 2, dtype=jnp.int32)
    inside = ((band_at >= 0) & (band_at < band_rows))[None, :, None, None]
    first_wide = condition(input_conv(input_padded, conv_in), cond_scale, cond_shift)
    first_wide = jnp.where(inside, first_wide, jnp.zeros_like(first_wide))
    first_hidden = first_wide[:, 2 : 2 + row_count]
    second_padded = jax.nn.gelu(feature_conv(first_wide, conv_mid)).astype(jnp.bfloat16)
    second_padded = jnp.where(inside[:, 1:-1], second_padded, jnp.zeros_like(second_padded))
    final_linear_response = feature_conv(second_padded, conv_out)
    latent_layer_three = (
        first_hidden.astype(jnp.float32) + jax.nn.gelu(final_linear_response)
    ).astype(jnp.bfloat16)
    final_layer_result = jnp.einsum(
        "mrwc,cv->vmrw", latent_layer_three, head_weight, preferred_element_type=jnp.float32
    )
    sample_prediction = (
        final_layer_result
        + jnp.transpose(upsampled_coarse, (1, 0, 2)).astype(jnp.float32)[:, None]
        + per_quantity_offset[:, None, None, None]
    ).astype(jnp.bfloat16)
    row_global = band_row[0] + tile_at * row_count + jnp.arange(row_count, dtype=jnp.int32)
    latitude = math.pi * (row_global.astype(jnp.float32) + 0.5) / GRID_ROWS - math.pi / 2
    row_factor = (jnp.cos(latitude) / (band_rows * col_count))[None, None, :, None]
    var_share = var_count // (lax.axis_size("group") * lax.axis_size("core"))
    var_start = lax.axis_index(MEMBER) * var_share
    collected_members = lax.all_to_all(
        sample_prediction, MEMBER, split_axis=0, concat_axis=1, tiled=True
    )
    sample_group_predictions = collected_members.astype(jnp.float32)
    member_count = sample_group_predictions.shape[1]
    truth = jnp.transpose(
        lax.dynamic_slice_in_dim(target, var_start, var_share, 1), (1, 0, 2)
    ).astype(jnp.float32)[:, None]
    pair_differ = sample_group_predictions[:, :, None] - sample_group_predictions[:, None, :]
    abs_sums = jnp.sum(jnp.abs(pair_differ), axis=2)
    sign_sums = jnp.sum(
        (pair_differ > 0).astype(jnp.float32) - (pair_differ < 0).astype(jnp.float32), axis=2
    )
    crps_share = jnp.mean(jnp.abs(sample_group_predictions - truth), axis=1) - jnp.sum(
        abs_sums, axis=1
    ) / (2 * member_count * (member_count - 1))
    crps_map = jnp.transpose(crps_share, (1, 0, 2))
    cot_share = (
        row_factor
        * (
            jnp.sign(sample_group_predictions - truth) / member_count
            - sign_sums / (member_count * (member_count - 1))
        )
    ).astype(jnp.bfloat16)
    cotangent = lax.all_to_all(cot_share, MEMBER, split_axis=1, concat_axis=0, tiled=True)
    head_grad = jnp.einsum(
        "mrwc,vmrw->cv", latent_layer_three, cotangent, preferred_element_type=jnp.float32
    )
    bias_grad = jnp.sum(cotangent.astype(jnp.float32), axis=(1, 2, 3))
    back = jnp.einsum("vmrw,cv->mrwc", cotangent, head_weight, preferred_element_type=jnp.float32)
    unused_out, pullback = jax.vjp(jax.nn.gelu, final_linear_response)
    d_pre = pullback(back)[0].astype(jnp.bfloat16)
    second_wide = jnp.pad(second_padded, ((0, 0), (0, 0), (1, 1), (0, 0)))
    rows_of = []
    for i in range(3):
        cols_of = []
        for j in range(3):
            cols_of.append(
                jnp.einsum(
                    "mrwc,mrwd->cd",
                    second_wide[:, i : i + row_count, j : j + col_count],
                    d_pre,
                    preferred_element_type=jnp.float32,
                )
            )
        rows_of.append(jnp.stack(cols_of))
    conv_grad = jnp.stack(rows_of)
    conv_grad, head_grad_t, bias_grad = all_reduce_sum((conv_grad, head_grad.T, bias_grad))
    head_grad = head_grad_t.T
    return (crps_map, conv_grad, head_grad, bias_grad)


def solution(mesh):
    members = mesh.shape["member"]
    split = Mesh(
        mesh.devices.reshape(members // 2, 2, mesh.shape["tile"]), ("group", "core", "tile")
    )
    return jax.shard_map(
        on_device,
        mesh=split,
        in_specs=(
            P("tile", None, None),
            P("tile", None, None),
            P(MEMBER),
            P(),
            P(),
            P(),
            P(),
            P(),
            P(),
            P(),
            P(),
        ),
        out_specs=(P("tile", MEMBER, None), P(), P(), P()),
        check_vma=False,
    )
```
